128 devices in a mesh: segment: 2 (over core), tensor: 4 (over x), batch: 16 (over z, y).
Axes of the slice: x: 4, y: 4, z: 4, core: 2. Of those that a mesh axis runs over, the one named last changes fastest.
Arguments:
- hidden: bfloat16 [3, 128, 16384], P(None, 'tensor', 'batch'), may hold values from -6 to 6
- norm_gain: bfloat16 [2, 16384], P('segment', 'batch'), may hold values from 0.25 to 1.75
- w_query: bfloat16 [2, 16384, 8192], P('segment', 'batch', 'tensor'), may hold values from -0.046875 to 0.046875
- key_value_weight: bfloat16 [2, 16384, 2048], P('segment', 'batch', 'tensor'), may hold values from -0.046875 to 0.046875
- w_out: bfloat16 [2, 8192, 16384], P('segment', 'tensor', 'batch'), may hold values from -0.0625 to 0.0625
- key_value_cache: bfloat16 [2, 32, 8, 256, 256], P('segment', 'batch', 'tensor'), may hold values from -6 to 6
- owner_slot: int32 [32], replicated, may hold values from 0 to 31, each once
- accepted: int32 [3, 32], replicated, may hold values from 1 to 4
Outputs:
- layer_outputs: bfloat16 [2, 3, 128, 16384], P('segment', None, 'tensor', 'batch')
- new_cache: bfloat16 [2, 32, 8, 12, 256], P('segment', 'batch', 'tensor')
The draws below stay inside these ranges and needn't reach their ends.
Inputs may be any that keep to these rules, and one draw needn't show every extreme that they name: `owner_slot`: each slot is held by exactly one request; slot s belongs to index s // 2 of batch.
All inputs are finite; a program needn't handle non-finite values.
Results may differ from the reference program's by a relative error of at most 0.0095.
Values may be sent and summed in bfloat16 or wider, within the bound.
No kernel may reach another device: no remote copies, remote signals or barrier semaphores. Data moves between devices by JAX's collectives and lax.ppermute only.
A program may use at most 64 MiB of HBM per device.

```python
import jax
import jax.numpy as jnp
from jax import lax

MODEL_WIDTH = 16384
HQ = 64
KEY_HEADS = 8
HEAD_SIZE = 128
DRAFT_BLOCK = 4
DECODE_ROUNDS = 3
CACHE_SLOTS = 256
GROUP_HEADS = 8
TARGET_LAYERS = 2
REQUEST_COUNT = 32
ROWS = 128


def with_ends(array, key, least, high):
    longest = array.shape.index(max(array.shape))
    spots = []
    for shift in (0, 1):
        where = [jax.random.randint(jax.random.fold_in(key, axis), (), 0, length) for axis, length in enumerate(array.shape)]
        where[longest] = (where[longest] + shift) % array.shape[longest]
        spots.append(tuple(where))
    return array.at[spots[0]].set(least).at[spots[1]].set(high)


def level_of(stream_key, dims, cuts, least, high):
    level = 1.0
    for axis_at, shards_of in cuts:
        heights = jax.random.uniform(jax.random.fold_in(jax.random.fold_in(stream_key, 6), axis_at), (shards_of,), jnp.float32, least / len(cuts), high / len(cuts))
        level = level * jnp.repeat(jnp.exp(heights), dims[axis_at] // shards_of).reshape((-1,) + (1,) * (len(dims) - 1 - axis_at))
    return level


def centred(stream_key, shape, spread, limit, split=(), dtype=jnp.bfloat16):
    result = jax.random.normal(stream_key, shape, jnp.float32) * spread
    if len(split) > 0:
        result = level_of(stream_key, shape, split, -0.22, 0.18) * result
    return jnp.clip(result, min=-limit, max=limit).astype(dtype)


def setup_inputs(seed: int = 0) -> dict:
    arg_keys = jax.random.split(jax.random.key(seed), 9)
    return {
        "hidden": centred(arg_keys[0], (DECODE_ROUNDS, ROWS, MODEL_WIDTH), 1.0, 6.0, ((1, 4), (2, 16))),
        "norm_gain": jnp.clip(1.0 + 0.15 * jax.random.normal(arg_keys[1], (TARGET_LAYERS, MODEL_WIDTH), jnp.float32), 0.25, 1.75).astype(jnp.bfloat16),
        "w_query": centred(arg_keys[2], (TARGET_LAYERS, MODEL_WIDTH, HQ * HEAD_SIZE), MODEL_WIDTH ** -0.5, 0.046875, ((0, 2), (1, 16), (2, 4))),
        "key_value_weight": centred(arg_keys[3], (TARGET_LAYERS, MODEL_WIDTH, 2 * KEY_HEADS * HEAD_SIZE), MODEL_WIDTH ** -0.5, 0.046875, ((0, 2), (1, 16), (2, 4))),
        "w_out": centred(arg_keys[4], (TARGET_LAYERS, HQ * HEAD_SIZE, MODEL_WIDTH), (HQ * HEAD_SIZE) ** -0.5, 0.0625, ((0, 2), (1, 4), (2, 16))),
        "key_value_cache": centred(arg_keys[5], (TARGET_LAYERS, REQUEST_COUNT, KEY_HEADS, CACHE_SLOTS, 2 * HEAD_SIZE), 1.0, 6.0, ((0, 2), (1, 16), (2, 4))),
        "owner_slot": jax.random.permutation(arg_keys[6], REQUEST_COUNT).astype(jnp.int32),
        "accepted": with_ends(jax.random.randint(arg_keys[7], (DECODE_ROUNDS, REQUEST_COUNT), 1, DRAFT_BLOCK + 1), jax.random.fold_in(arg_keys[7], 1), 1, DRAFT_BLOCK).astype(jnp.int32),
    }


def reference(hidden, norm_gain, w_query, key_value_weight, w_out, key_value_cache, owner_slot, accepted):
    scale = HEAD_SIZE ** (-0.5)
    positions = jnp.arange(DECODE_ROUNDS * DRAFT_BLOCK)
    round_of = positions // DRAFT_BLOCK
    place = positions % DRAFT_BLOCK
    inverse = jnp.argsort(owner_slot).astype(jnp.int32)
    extended_all = [jnp.zeros((REQUEST_COUNT, KEY_HEADS, DECODE_ROUNDS * DRAFT_BLOCK, 2 * HEAD_SIZE), jnp.bfloat16) for layer_current in range(TARGET_LAYERS)]
    outs_all = [[None] * DECODE_ROUNDS for layer_current in range(TARGET_LAYERS)]
    causal = jnp.arange(DRAFT_BLOCK)[None, :] <= jnp.arange(DRAFT_BLOCK)[:, None]
    for rnd in range(DECODE_ROUNDS):
        x = hidden[rnd]
        for layer_current in range(TARGET_LAYERS):
            xf = x.astype(jnp.float32)
            total = lax.optimization_barrier(jnp.sum(xf * xf, axis=1))
            normed = (xf * lax.rsqrt(total / MODEL_WIDTH + 1e-05)[:, None] * norm_gain[layer_current].astype(jnp.float32)).astype(jnp.bfloat16)
            query_rows_new = jnp.dot(normed, w_query[layer_current], preferred_element_type=jnp.float32).astype(jnp.bfloat16)
            key_value_rows = jnp.dot(normed, key_value_weight[layer_current], preferred_element_type=jnp.float32).astype(jnp.bfloat16)
            query_heads = query_rows_new.reshape(REQUEST_COUNT, DRAFT_BLOCK, KEY_HEADS, GROUP_HEADS, HEAD_SIZE).astype(jnp.float32)
            fresh_key_value = key_value_rows.reshape(REQUEST_COUNT, DRAFT_BLOCK, KEY_HEADS, 2 * HEAD_SIZE).transpose(0, 2, 1, 3)
            cache_req = key_value_cache[layer_current][owner_slot]
            ext_req = extended_all[layer_current][owner_slot]
            keys_all = jnp.concatenate([cache_req, ext_req, fresh_key_value], axis=2).astype(jnp.float32)
            ext_valid = (round_of[None, :] < rnd) & (place[None, :] < accepted[:, :].T[:, round_of])
            mask = jnp.concatenate([jnp.ones((REQUEST_COUNT, DRAFT_BLOCK, CACHE_SLOTS), bool), jnp.broadcast_to(ext_valid[:, None, :], (REQUEST_COUNT, DRAFT_BLOCK, DECODE_ROUNDS * DRAFT_BLOCK)), jnp.broadcast_to(causal[None], (REQUEST_COUNT, DRAFT_BLOCK, DRAFT_BLOCK))], axis=2)
            scores = jnp.einsum('qjhgd,qhld->qhgjl', query_heads, keys_all[..., :HEAD_SIZE]) * scale
            scores = jnp.where(mask[:, None, None], scores, -1e+30)
            weights = jax.nn.softmax(scores, axis=-1).astype(jnp.bfloat16)
            attended = jnp.einsum('qhgjl,qhld->qjhgd', weights.astype(jnp.float32), keys_all[..., HEAD_SIZE:])
            attended = attended.astype(jnp.bfloat16).reshape(ROWS, HQ * HEAD_SIZE)
            delta = jnp.dot(attended, w_out[layer_current], preferred_element_type=jnp.float32)
            x = (xf + delta).astype(jnp.bfloat16)
            outs_all[layer_current][rnd] = x
            keep = jnp.arange(DRAFT_BLOCK)[None, :] < accepted[rnd][:, None]
            masked = jnp.where(keep[:, None, :, None], fresh_key_value, jnp.zeros_like(fresh_key_value))
            ext_new = ext_req.at[:, :, rnd * DRAFT_BLOCK:(rnd + 1) * DRAFT_BLOCK].set(masked)
            extended_all[layer_current] = ext_new[inverse]
    layer_outputs = jnp.stack([jnp.stack(outs_all[layer_current]) for layer_current in range(TARGET_LAYERS)])
    new_cache = jnp.stack(extended_all)
    return (layer_outputs, new_cache)
```

```python
import jax
import jax.numpy as jnp
from jax import lax
from jax.sharding import PartitionSpec as P

MODEL_WIDTH = 16384
HEAD_SIZE = 128
DRAFT_BLOCK = 4
DECODE_ROUNDS = 3
GROUP_HEADS = 8
EXTRA = 128


def passed_along(block, axis, distance):
    devices = range(lax.axis_size(axis))
    route = [(i - distance, i) for i in devices if i - distance in devices]
    return lax.ppermute(block, axis, route)


def shards(
    hidden, norm_gain, w_query, key_value_weight, w_out, key_value_cache, owner_slot, accepted
):
    f32, bf16 = jnp.float32, jnp.bfloat16
    rounds, rows_local, width_local = hidden.shape
    n_segment = lax.axis_size("segment")
    segment = lax.axis_index("segment")
    tensor = lax.axis_index("tensor")
    group = lax.axis_index("batch")
    requests = owner_slot.shape[0]
    rows_total = requests * DRAFT_BLOCK
    slots_local = key_value_cache.shape[1]
    kv_local = key_value_cache.shape[2]
    query_cols = w_query.shape[2]
    kv_cols = key_value_weight.shape[2]
    block = rounds * DRAFT_BLOCK
    own_rows = slots_local * block
    req_local = rows_local // DRAFT_BLOCK
    scale = HEAD_SIZE ** (-0.5)
    gain = norm_gain[0].astype(f32)
    cache_local = key_value_cache[0]

    onehot = (owner_slot[None, :] == jnp.arange(requests)[:, None]).astype(jnp.int32)
    inverse = jnp.sum(onehot * jnp.arange(requests)[None, :], axis=1)
    acc_slot = jnp.sum(onehot[None] * accepted[:, None, :], axis=2)
    acc_own = lax.dynamic_slice_in_dim(acc_slot, group * slots_local, slots_local, 1)

    rr = jnp.arange(rounds)
    jj = jnp.arange(DRAFT_BLOCK)
    sort_index = (
        rr[None, :, None] * rows_total + inverse[:, None, None] * DRAFT_BLOCK + jj[None, None, :]
    ).reshape(-1)
    own_req = tensor * req_local + jnp.arange(req_local)
    own_index = (
        owner_slot[own_req][None, :, None] * block + rr[:, None, None] * DRAFT_BLOCK + jj[None, None, :]
    ).reshape(-1)

    pos = jnp.arange(block)
    r2 = pos // DRAFT_BLOCK
    place = pos % DRAFT_BLOCK
    acc_pos = acc_own[r2, :].T
    earlier = (r2[None, None, None, :] < rr[None, :, None, None]) & (
        place[None, None, None, :] < acc_pos[:, None, None, :]
    )
    same = (r2[None, :] == rr[:, None])[:, None, :] & (place[None, None, :] <= jj[None, :, None])
    valid = earlier | same[None]
    keep = place[None, :] < acc_pos

    def layer(x_sorted):
        xf = x_sorted.astype(f32)
        sq = jnp.sum(xf * xf, axis=1, keepdims=True)
        xg = (xf * gain[None, :]).astype(bf16)
        first = jnp.dot(xg, w_query[0], preferred_element_type=f32)
        second = jnp.dot(xg, key_value_weight[0], preferred_element_type=f32)
        proj = jnp.concatenate(
            [first, second, jnp.broadcast_to(sq, (sq.shape[0], EXTRA))], axis=1
        )
        proj = lax.psum_scatter(proj, "batch", scatter_dimension=0, tiled=True)
        inv = lax.rsqrt(proj[:, query_cols + kv_cols :][:, :1] / MODEL_WIDTH + 1e-05)
        query = (proj[:, :query_cols] * inv).astype(bf16)
        keyval = (proj[:, query_cols : query_cols + kv_cols] * inv).astype(bf16)
        query_heads = query.reshape(
            slots_local, rounds, DRAFT_BLOCK, kv_local, GROUP_HEADS, HEAD_SIZE
        )
        fresh = keyval.reshape(slots_local, block, kv_local, 2 * HEAD_SIZE).transpose(0, 2, 1, 3)
        s_cache = jnp.einsum(
            "srjhgd,shld->shgrjl", query_heads, cache_local[..., :HEAD_SIZE],
            preferred_element_type=f32,
        ) * scale
        s_fresh = jnp.einsum(
            "srjhgd,shld->shgrjl", query_heads, fresh[..., :HEAD_SIZE],
            preferred_element_type=f32,
        ) * scale
        s_fresh = jnp.where(valid[:, None, None], s_fresh, -1e30)
        scores = jnp.concatenate([s_cache, s_fresh], axis=-1)
        weights = jax.nn.softmax(scores, axis=-1).astype(bf16)
        values = jnp.concatenate([cache_local[..., HEAD_SIZE:], fresh[..., HEAD_SIZE:]], axis=2)
        attended = jnp.einsum(
            "shgrjl,shld->srjhgd", weights, values, preferred_element_type=f32
        )
        attended = attended.astype(bf16).reshape(own_rows, query_cols)
        gathered = lax.all_gather(attended, "batch", axis=0, tiled=True)
        partial = jnp.dot(gathered, w_out[0], preferred_element_type=f32)
        summed = lax.psum(partial.astype(bf16), "tensor").astype(f32)
        x_new = (xf + summed).astype(bf16)
        ext_new = jnp.where(keep[:, None, :, None], fresh, jnp.zeros_like(fresh))
        return x_new, ext_new

    rows_all = lax.all_gather(hidden, "tensor", axis=1, tiled=True).reshape(-1, width_local)
    x = jnp.take(rows_all, sort_index, axis=0)
    record = None
    ext = None
    for step in range(n_segment):
        x_new, ext_new = layer(x)
        rec_new = jnp.take(x_new, own_index, axis=0).reshape(rounds, rows_local, width_local)
        if step == 0:
            record, ext = rec_new, ext_new
        else:
            active = segment == step
            record = jnp.where(active, rec_new, record)
            ext = jnp.where(active, ext_new, ext)
        if step + 1 < n_segment:
            x = passed_along(x_new, "segment", 1)
    return (record[None], ext[None])


def solution(mesh):
    in_specs = (
        P(None, "tensor", "batch"),
        P("segment", "batch"),
        P("segment", "batch", "tensor"),
        P("segment", "batch", "tensor"),
        P("segment", "tensor", "batch"),
        P("segment", "batch", "tensor", None, None),
        P(),
        P(),
    )
    out_specs = (P("segment", None, "tensor", "batch"), P("segment", "batch", "tensor", None, None))
    return jax.shard_map(shards, mesh=mesh, in_specs=in_specs, out_specs=out_specs, check_vma=False)
```

```python
import jax
import jax.numpy as jnp
from jax import lax
from jax.sharding import PartitionSpec as P

MODEL_WIDTH = 16384
HEAD_SIZE = 128
DRAFT_BLOCK = 4
DECODE_ROUNDS = 3
GROUP_HEADS = 8


BATCH_INNER = 4


def shifted(x, axis, fn):
    n = lax.axis_size(axis)
    return lax.ppermute(x, axis, [(i, fn(i, n)) for i in range(n)])


def along_tensor(x, k):
    return shifted(x, "tensor", lambda i, n: (i + k) % n)


def along_y(x, k):
    m = BATCH_INNER
    return shifted(x, "batch", lambda i, n: (i // m) * m + (i % m + k) % m)


def along_z(x, k):
    m = BATCH_INNER
    return shifted(x, "batch", lambda i, n: ((i // m + k) % (n // m)) * m + i % m)


def spread(blocks, pos, send):
    m = blocks.shape[0]
    out = [lax.dynamic_index_in_dim(blocks, pos, 0, keepdims=False)]
    for k in range(1, m):
        piece = lax.dynamic_index_in_dim(blocks, (pos + k) % m, 0, keepdims=False)
        out.append(send(piece, k))
    return out


def gather_from(x, pos, m, send):
    out = [x] + [send(x, k) for k in range(1, m)]
    order = (pos - jnp.arange(m)) % m
    return jnp.take(jnp.stack(out), order, axis=0)


def passed_along(block, axis, distance):
    devices = range(lax.axis_size(axis))
    route = [(i - distance, i) for i in devices if i - distance in devices]
    return lax.ppermute(block, axis, route)


def shards(
    hidden, norm_gain, w_query, key_value_weight, w_out, key_value_cache, owner_slot, accepted
):
    f32, bf16 = jnp.float32, jnp.bfloat16
    rounds, rows_local, width_local = hidden.shape
    n_segment = lax.axis_size("segment")
    segment = lax.axis_index("segment")
    tensor = lax.axis_index("tensor")
    group = lax.axis_index("batch")
    requests = owner_slot.shape[0]
    rows_total = requests * DRAFT_BLOCK
    slots_local = key_value_cache.shape[1]
    kv_local = key_value_cache.shape[2]
    query_cols = w_query.shape[2]
    kv_cols = key_value_weight.shape[2]
    block = rounds * DRAFT_BLOCK
    own_rows = slots_local * block
    req_local = rows_local // DRAFT_BLOCK
    scale = HEAD_SIZE ** (-0.5)
    gain = norm_gain[0].astype(f32)
    cache_local = key_value_cache[0]

    onehot = (owner_slot[None, :] == jnp.arange(requests)[:, None]).astype(jnp.int32)
    inverse = jnp.sum(onehot * jnp.arange(requests)[None, :], axis=1)
    acc_slot = jnp.sum(onehot[None] * accepted[:, None, :], axis=2)
    acc_own = lax.dynamic_slice_in_dim(acc_slot, group * slots_local, slots_local, 1)

    rr = jnp.arange(rounds)
    jj = jnp.arange(DRAFT_BLOCK)
    sort_index = (
        rr[None, :, None] * rows_total + inverse[:, None, None] * DRAFT_BLOCK + jj[None, None, :]
    ).reshape(-1)
    own_req = tensor * req_local + jnp.arange(req_local)
    own_index = (
        owner_slot[own_req][None, :, None] * block + rr[:, None, None] * DRAFT_BLOCK + jj[None, None, :]
    ).reshape(-1)

    pos = jnp.arange(block)
    r2 = pos // DRAFT_BLOCK
    place = pos % DRAFT_BLOCK
    acc_pos = acc_own[r2, :].T
    earlier = (r2[None, None, None, :] < rr[None, :, None, None]) & (
        place[None, None, None, :] < acc_pos[:, None, None, :]
    )
    same = (r2[None, :] == rr[:, None])[:, None, :] & (place[None, None, :] <= jj[None, :, None])
    valid = earlier | same[None]
    keep = place[None, :] < acc_pos

    n_tensor = lax.axis_size("tensor")
    n_y = BATCH_INNER
    n_z = lax.axis_size("batch") // n_y
    z_pos = group // n_y
    y_pos = group % n_y

    def layer(x_sorted):
        xf = x_sorted.astype(f32)
        sq = jnp.sum(xf * xf, axis=1)
        xg = (xf * gain[None, :]).astype(bf16)
        first = jnp.dot(xg, w_query[0], preferred_element_type=f32)
        second = jnp.dot(xg, key_value_weight[0], preferred_element_type=f32)
        proj = jnp.concatenate([first, second], axis=1)
        cols = proj.shape[1]
        by_y = proj.astype(bf16).reshape(n_z, n_y, own_rows, cols).transpose(1, 0, 2, 3)
        sq_y = sq.reshape(n_z, n_y, own_rows).transpose(1, 0, 2)
        part = sum(r.astype(f32) for r in spread(by_y, y_pos, along_y))
        part_sq = sum(spread(sq_y, y_pos, along_y))
        total = sum(spread(part, z_pos, along_z))
        total_sq = sum(spread(part_sq, z_pos, along_z))
        inv = lax.rsqrt(total_sq / MODEL_WIDTH + 1e-05)[:, None]
        query = (total[:, :query_cols] * inv).astype(bf16)
        keyval = (total[:, query_cols:] * inv).astype(bf16)
        query_heads = query.reshape(
            slots_local, rounds, DRAFT_BLOCK, kv_local, GROUP_HEADS, HEAD_SIZE
        )
        fresh = keyval.reshape(slots_local, block, kv_local, 2 * HEAD_SIZE).transpose(0, 2, 1, 3)
        s_cache = jnp.einsum(
            "srjhgd,shld->shgrjl", query_heads, cache_local[..., :HEAD_SIZE],
            preferred_element_type=f32,
        ) * scale
        s_fresh = jnp.einsum(
            "srjhgd,shld->shgrjl", query_heads, fresh[..., :HEAD_SIZE],
            preferred_element_type=f32,
        ) * scale
        s_fresh = jnp.where(valid[:, None, None], s_fresh, -1e30)
        scores = jnp.concatenate([s_cache, s_fresh], axis=-1)
        weights = jax.nn.softmax(scores, axis=-1).astype(bf16)
        values = jnp.concatenate([cache_local[..., HEAD_SIZE:], fresh[..., HEAD_SIZE:]], axis=2)
        attended = jnp.einsum(
            "shgrjl,shld->srjhgd", weights, values, preferred_element_type=f32
        )
        attended = attended.astype(bf16).reshape(own_rows, query_cols)
        by_z = gather_from(attended, z_pos, n_z, along_z)
        by_zy = gather_from(by_z, y_pos, n_y, along_y)
        gathered = by_zy.transpose(1, 0, 2, 3).reshape(-1, query_cols)
        partial = jnp.dot(gathered, w_out[0], preferred_element_type=f32)
        quarter = partial.shape[0] // n_tensor
        pieces = partial.astype(bf16).reshape(n_tensor, quarter, width_local)
        mine = sum(r.astype(f32) for r in spread(pieces, tensor, along_tensor))
        x_mine = lax.dynamic_index_in_dim(
            xf.reshape(n_tensor, quarter, width_local), tensor, 0, keepdims=False
        )
        x_mine = (x_mine + mine).astype(bf16)
        x_new = gather_from(x_mine, tensor, n_tensor, along_tensor).reshape(-1, width_local)
        ext_new = jnp.where(keep[:, None, :, None], fresh, jnp.zeros_like(fresh))
        return x_new, ext_new

    rows_all = gather_from(hidden, tensor, n_tensor, along_tensor)
    rows_all = rows_all.transpose(1, 0, 2, 3).reshape(-1, width_local)
    x = jnp.take(rows_all, sort_index, axis=0)
    record = None
    ext = None
    for step in range(n_segment):
        x_new, ext_new = layer(x)
        rec_new = jnp.take(x_new, own_index, axis=0).reshape(rounds, rows_local, width_local)
        if step == 0:
            record, ext = rec_new, ext_new
        else:
            active = segment == step
            record = jnp.where(active, rec_new, record)
            ext = jnp.where(active, ext_new, ext)
        if step + 1 < n_segment:
            x = passed_along(x_new, "segment", 1)
    return (record[None], ext[None])


def solution(mesh):
    in_specs = (
        P(None, "tensor", "batch"),
        P("segment", "batch"),
        P("segment", "batch", "tensor"),
        P("segment", "batch", "tensor"),
        P("segment", "tensor", "batch"),
        P("segment", "batch", "tensor", None, None),
        P(),
        P(),
    )
    out_specs = (P("segment", None, "tensor", "batch"), P("segment", "batch", "tensor", None, None))
    return jax.shard_map(shards, mesh=mesh, in_specs=in_specs, out_specs=out_specs, check_vma=False)
```

```python
import jax
import jax.numpy as jnp
from jax import lax
from jax.sharding import PartitionSpec as P

MODEL_WIDTH = 16384
HEAD_SIZE = 128
DRAFT_BLOCK = 4
DECODE_ROUNDS = 3
GROUP_HEADS = 8


BATCH_INNER = 4


def shifted(x, axis, fn):
    n = lax.axis_size(axis)
    return lax.ppermute(x, axis, [(i, fn(i, n)) for i in range(n)])


def along_tensor(x, k):
    return shifted(x, "tensor", lambda i, n: (i + k) % n)


def along_y(x, k):
    m = BATCH_INNER
    return shifted(x, "batch", lambda i, n: (i // m) * m + (i % m + k) % m)


def along_z(x, k):
    m = BATCH_INNER
    return shifted(x, "batch", lambda i, n: ((i // m + k) % (n // m)) * m + i % m)


def spread(blocks, pos, send):
    m = blocks.shape[0]
    out = [lax.dynamic_index_in_dim(blocks, pos, 0, keepdims=False)]
    for k in range(1, m):
        piece = lax.dynamic_index_in_dim(blocks, (pos + k) % m, 0, keepdims=False)
        out.append(send(piece, k))
    return out


def gather_from(x, pos, m, send):
    out = [x] + [send(x, k) for k in range(1, m)]
    order = (pos - jnp.arange(m)) % m
    return jnp.take(jnp.stack(out), order, axis=0)


def passed_along(block, axis, distance):
    devices = range(lax.axis_size(axis))
    route = [(i - distance, i) for i in devices if i - distance in devices]
    return lax.ppermute(block, axis, route)


def shards(
    hidden, norm_gain, w_query, key_value_weight, w_out, key_value_cache, owner_slot, accepted
):
    f32, bf16 = jnp.float32, jnp.bfloat16
    rounds, rows_local, width_local = hidden.shape
    n_segment = lax.axis_size("segment")
    segment = lax.axis_index("segment")
    tensor = lax.axis_index("tensor")
    group = lax.axis_index("batch")
    requests = owner_slot.shape[0]
    rows_total = requests * DRAFT_BLOCK
    slots_local = key_value_cache.shape[1]
    kv_local = key_value_cache.shape[2]
    query_cols = w_query.shape[2]
    kv_cols = key_value_weight.shape[2]
    block = rounds * DRAFT_BLOCK
    own_rows = slots_local * block
    req_local = rows_local // DRAFT_BLOCK
    scale = HEAD_SIZE ** (-0.5)
    gain = norm_gain[0].astype(f32)
    cache_local = key_value_cache[0]

    onehot = (owner_slot[None, :] == jnp.arange(requests)[:, None]).astype(jnp.int32)
    inverse = jnp.sum(onehot * jnp.arange(requests)[None, :], axis=1)
    acc_slot = jnp.sum(onehot[None] * accepted[:, None, :], axis=2)
    acc_own = lax.dynamic_slice_in_dim(acc_slot, group * slots_local, slots_local, 1)

    rr = jnp.arange(rounds)
    jj = jnp.arange(DRAFT_BLOCK)
    sort_index = (
        rr[None, :, None] * rows_total + inverse[:, None, None] * DRAFT_BLOCK + jj[None, None, :]
    ).reshape(-1)
    own_req = tensor * req_local + jnp.arange(req_local)
    own_index = (
        owner_slot[own_req][None, :, None] * block + rr[:, None, None] * DRAFT_BLOCK + jj[None, None, :]
    ).reshape(-1)

    pos = jnp.arange(block)
    r2 = pos // DRAFT_BLOCK
    place = pos % DRAFT_BLOCK
    acc_pos = acc_own[r2, :].T
    earlier = (r2[None, None, None, :] < rr[None, :, None, None]) & (
        place[None, None, None, :] < acc_pos[:, None, None, :]
    )
    same = (r2[None, :] == rr[:, None])[:, None, :] & (place[None, None, :] <= jj[None, :, None])
    valid = earlier | same[None]
    keep = place[None, :] < acc_pos

    n_tensor = lax.axis_size("tensor")
    n_y = BATCH_INNER
    n_z = lax.axis_size("batch") // n_y
    z_pos = group // n_y
    y_pos = group % n_y

    back_index = (
        owner_slot[None, :, None] * block + rr[:, None, None] * DRAFT_BLOCK + jj[None, None, :]
    ).reshape(-1)

    def layer(x_sorted, last):
        xf = x_sorted.astype(f32)
        sq = jnp.sum(xf * xf, axis=1, keepdims=True)
        sq_hi = sq.astype(bf16)
        sq_lo = (sq - sq_hi.astype(f32)).astype(bf16)
        xg = (xf * gain[None, :]).astype(bf16)
        first = jnp.dot(xg, w_query[0], preferred_element_type=f32)
        second = jnp.dot(xg, key_value_weight[0], preferred_element_type=f32)
        proj = jnp.concatenate([first.astype(bf16), second.astype(bf16), sq_hi, sq_lo], axis=1)
        cols = proj.shape[1]
        by_y = proj.reshape(n_z, n_y, own_rows, cols).transpose(1, 0, 2, 3)
        part = sum(r.astype(f32) for r in spread(by_y, y_pos, along_y))
        total = sum(spread(part, z_pos, along_z))
        total_sq = total[:, query_cols + kv_cols] + total[:, query_cols + kv_cols + 1]
        inv = lax.rsqrt(total_sq / MODEL_WIDTH + 1e-05)[:, None]
        query = (total[:, :query_cols] * inv).astype(bf16)
        keyval = (total[:, query_cols : query_cols + kv_cols] * inv).astype(bf16)
        query_heads = query.reshape(
            slots_local, rounds, DRAFT_BLOCK, kv_local, GROUP_HEADS, HEAD_SIZE
        )
        fresh = keyval.reshape(slots_local, block, kv_local, 2 * HEAD_SIZE).transpose(0, 2, 1, 3)
        s_cache = jnp.einsum(
            "srjhgd,shld->shgrjl", query_heads, cache_local[..., :HEAD_SIZE],
            preferred_element_type=f32,
        ) * scale
        s_fresh = jnp.einsum(
            "srjhgd,shld->shgrjl", query_heads, fresh[..., :HEAD_SIZE],
            preferred_element_type=f32,
        ) * scale
        s_fresh = jnp.where(valid[:, None, None], s_fresh, -1e30)
        scores = jnp.concatenate([s_cache, s_fresh], axis=-1)
        weights = jax.nn.softmax(scores, axis=-1).astype(bf16)
        values = jnp.concatenate([cache_local[..., HEAD_SIZE:], fresh[..., HEAD_SIZE:]], axis=2)
        attended = jnp.einsum(
            "shgrjl,shld->srjhgd", weights, values, preferred_element_type=f32
        )
        attended = attended.astype(bf16).reshape(own_rows, query_cols)
        by_z = gather_from(attended, z_pos, n_z, along_z)
        by_zy = gather_from(by_z, y_pos, n_y, along_y)
        gathered = by_zy.transpose(1, 0, 2, 3).reshape(-1, query_cols)
        partial = jnp.dot(gathered, w_out[0], preferred_element_type=f32)
        ext_new = jnp.where(keep[:, None, :, None], fresh, jnp.zeros_like(fresh))
        if last:
            natural = jnp.take(partial.astype(bf16), back_index, axis=0)
            pieces = natural.reshape(rounds, n_tensor, rows_local, width_local).transpose(1, 0, 2, 3)
            mine = sum(r.astype(f32) for r in spread(pieces, tensor, along_tensor))
            x_own = jnp.take(xf, own_index, axis=0).reshape(rounds, rows_local, width_local)
            return None, (x_own + mine).astype(bf16), ext_new
        quarter = partial.shape[0] // n_tensor
        pieces = partial.astype(bf16).reshape(n_tensor, quarter, width_local)
        mine = sum(r.astype(f32) for r in spread(pieces, tensor, along_tensor))
        x_mine = lax.dynamic_index_in_dim(
            xf.reshape(n_tensor, quarter, width_local), tensor, 0, keepdims=False
        )
        x_mine = (x_mine + mine).astype(bf16)
        x_new = gather_from(x_mine, tensor, n_tensor, along_tensor).reshape(-1, width_local)
        rec_new = jnp.take(x_new, own_index, axis=0).reshape(rounds, rows_local, width_local)
        return x_new, rec_new, ext_new

    rows_all = gather_from(hidden, tensor, n_tensor, along_tensor)
    rows_all = rows_all.transpose(1, 0, 2, 3).reshape(-1, width_local)
    x = jnp.take(rows_all, sort_index, axis=0)
    record = None
    ext = None
    for step in range(n_segment):
        x_new, rec_new, ext_new = layer(x, step + 1 == n_segment)
        if step == 0:
            record, ext = rec_new, ext_new
        else:
            active = segment == step
            record = jnp.where(active, rec_new, record)
            ext = jnp.where(active, ext_new, ext)
        if step + 1 < n_segment:
            x = passed_along(x_new, "segment", 1)
    return (record[None], ext[None])


def solution(mesh):
    in_specs = (
        P(None, "tensor", "batch"),
        P("segment", "batch"),
        P("segment", "batch", "tensor"),
        P("segment", "batch", "tensor"),
        P("segment", "tensor", "batch"),
        P("segment", "batch", "tensor", None, None),
        P(),
        P(),
    )
    out_specs = (P("segment", None, "tensor", "batch"), P("segment", "batch", "tensor", None, None))
    return jax.shard_map(shards, mesh=mesh, in_specs=in_specs, out_specs=out_specs, check_vma=False)
```

```python
import jax
import jax.numpy as jnp
from jax import lax
from jax.sharding import PartitionSpec as P

MODEL_WIDTH = 16384
HEAD_SIZE = 128
DRAFT_BLOCK = 4
DECODE_ROUNDS = 3
GROUP_HEADS = 8


BATCH_INNER = 4


def shifted(x, axis, fn, active):
    n = lax.axis_size(axis)
    pairs = [(active * n + i, active * n + fn(i, n)) for i in range(n)]
    return lax.ppermute(x, ("segment", axis), pairs)


def along_tensor(active):
    return lambda x, k: shifted(x, "tensor", lambda i, n: (i + k) % n, active)


def along_y(active):
    m = BATCH_INNER
    return lambda x, k: shifted(
        x, "batch", lambda i, n: (i // m) * m + (i % m + k) % m, active
    )


def along_z(active):
    m = BATCH_INNER
    return lambda x, k: shifted(
        x, "batch", lambda i, n: ((i // m + k) % (n // m)) * m + i % m, active
    )


def spread(blocks, pos, send):
    m = blocks.shape[0]
    out = [lax.dynamic_index_in_dim(blocks, pos, 0, keepdims=False)]
    for k in range(1, m):
        piece = lax.dynamic_index_in_dim(blocks, (pos + k) % m, 0, keepdims=False)
        out.append(send(piece, k))
    return out


def gather_from(x, pos, m, send):
    out = [x] + [send(x, k) for k in range(1, m)]
    order = (pos - jnp.arange(m)) % m
    return jnp.take(jnp.stack(out), order, axis=0)


def passed_along(block, axis, distance):
    devices = range(lax.axis_size(axis))
    route = [(i - distance, i) for i in devices if i - distance in devices]
    return lax.ppermute(block, axis, route)


def shards(
    hidden, norm_gain, w_query, key_value_weight, w_out, key_value_cache, owner_slot, accepted
):
    f32, bf16 = jnp.float32, jnp.bfloat16
    rounds, rows_local, width_local = hidden.shape
    n_segment = lax.axis_size("segment")
    segment = lax.axis_index("segment")
    tensor = lax.axis_index("tensor")
    group = lax.axis_index("batch")
    requests = owner_slot.shape[0]
    rows_total = requests * DRAFT_BLOCK
    slots_local = key_value_cache.shape[1]
    kv_local = key_value_cache.shape[2]
    query_cols = w_query.shape[2]
    kv_cols = key_value_weight.shape[2]
    block = rounds * DRAFT_BLOCK
    own_rows = slots_local * block
    req_local = rows_local // DRAFT_BLOCK
    scale = HEAD_SIZE ** (-0.5)
    gain = norm_gain[0].astype(f32)
    cache_local = key_value_cache[0]

    onehot = (owner_slot[None, :] == jnp.arange(requests)[:, None]).astype(jnp.int32)
    inverse = jnp.sum(onehot * jnp.arange(requests)[None, :], axis=1)
    acc_slot = jnp.sum(onehot[None] * accepted[:, None, :], axis=2)
    acc_own = lax.dynamic_slice_in_dim(acc_slot, group * slots_local, slots_local, 1)

    rr = jnp.arange(rounds)
    jj = jnp.arange(DRAFT_BLOCK)
    sort_index = (
        rr[None, :, None] * rows_total + inverse[:, None, None] * DRAFT_BLOCK + jj[None, None, :]
    ).reshape(-1)
    own_req = tensor * req_local + jnp.arange(req_local)
    own_index = (
        owner_slot[own_req][None, :, None] * block + rr[:, None, None] * DRAFT_BLOCK + jj[None, None, :]
    ).reshape(-1)

    pos = jnp.arange(block)
    r2 = pos // DRAFT_BLOCK
    place = pos % DRAFT_BLOCK
    acc_pos = acc_own[r2, :].T
    earlier = (r2[None, None, None, :] < rr[None, :, None, None]) & (
        place[None, None, None, :] < acc_pos[:, None, None, :]
    )
    same = (r2[None, :] == rr[:, None])[:, None, :] & (place[None, None, :] <= jj[None, :, None])
    valid = earlier | same[None]
    keep = place[None, :] < acc_pos

    n_tensor = lax.axis_size("tensor")
    n_y = BATCH_INNER
    n_z = lax.axis_size("batch") // n_y
    z_pos = group // n_y
    y_pos = group % n_y

    back_index = (
        owner_slot[None, :, None] * block + rr[:, None, None] * DRAFT_BLOCK + jj[None, None, :]
    ).reshape(-1)

    def layer(x_sorted, last, active):
        send_t, send_y, send_z = along_tensor(active), along_y(active), along_z(active)
        xf = x_sorted.astype(f32)
        sq = jnp.sum(xf * xf, axis=1, keepdims=True)
        sq_hi = sq.astype(bf16)
        sq_lo = (sq - sq_hi.astype(f32)).astype(bf16)
        xg = (xf * gain[None, :]).astype(bf16)
        first = jnp.dot(xg, w_query[0], preferred_element_type=f32)
        second = jnp.dot(xg, key_value_weight[0], preferred_element_type=f32)
        proj = jnp.concatenate([first.astype(bf16), second.astype(bf16), sq_hi, sq_lo], axis=1)
        cols = proj.shape[1]
        by_y = proj.reshape(n_z, n_y, own_rows, cols).transpose(1, 0, 2, 3)
        part = sum(r.astype(f32) for r in spread(by_y, y_pos, send_y))
        total = sum(spread(part, z_pos, send_z))
        total_sq = total[:, query_cols + kv_cols] + total[:, query_cols + kv_cols + 1]
        inv = lax.rsqrt(total_sq / MODEL_WIDTH + 1e-05)[:, None]
        query = (total[:, :query_cols] * inv).astype(bf16)
        keyval = (total[:, query_cols : query_cols + kv_cols] * inv).astype(bf16)
        query_heads = query.reshape(
            slots_local, rounds, DRAFT_BLOCK, kv_local, GROUP_HEADS, HEAD_SIZE
        )
        fresh = keyval.reshape(slots_local, block, kv_local, 2 * HEAD_SIZE).transpose(0, 2, 1, 3)
        s_cache = jnp.einsum(
            "srjhgd,shld->shgrjl", query_heads, cache_local[..., :HEAD_SIZE],
            preferred_element_type=f32,
        ) * scale
        s_fresh = jnp.einsum(
            "srjhgd,shld->shgrjl", query_heads, fresh[..., :HEAD_SIZE],
            preferred_element_type=f32,
        ) * scale
        s_fresh = jnp.where(valid[:, None, None], s_fresh, -1e30)
        scores = jnp.concatenate([s_cache, s_fresh], axis=-1)
        weights = jax.nn.softmax(scores, axis=-1).astype(bf16)
        values = jnp.concatenate([cache_local[..., HEAD_SIZE:], fresh[..., HEAD_SIZE:]], axis=2)
        attended = jnp.einsum(
            "shgrjl,shld->srjhgd", weights, values, preferred_element_type=f32
        )
        attended = attended.astype(bf16).reshape(own_rows, query_cols)
        by_z = gather_from(attended, z_pos, n_z, send_z)
        by_zy = gather_from(by_z, y_pos, n_y, send_y)
        gathered = by_zy.transpose(1, 0, 2, 3).reshape(-1, query_cols)
        partial = jnp.dot(gathered, w_out[0], preferred_element_type=f32)
        ext_new = jnp.where(keep[:, None, :, None], fresh, jnp.zeros_like(fresh))
        if last:
            natural = jnp.take(partial.astype(bf16), back_index, axis=0)
            pieces = natural.reshape(rounds, n_tensor, rows_local, width_local).transpose(1, 0, 2, 3)
            mine = sum(r.astype(f32) for r in spread(pieces, tensor, send_t))
            x_own = jnp.take(xf, own_index, axis=0).reshape(rounds, rows_local, width_local)
            return None, (x_own + mine).astype(bf16), ext_new
        quarter = partial.shape[0] // n_tensor
        pieces = partial.astype(bf16).reshape(n_tensor, quarter, width_local)
        mine = sum(r.astype(f32) for r in spread(pieces, tensor, send_t))
        x_mine = lax.dynamic_index_in_dim(
            xf.reshape(n_tensor, quarter, width_local), tensor, 0, keepdims=False
        )
        x_mine = (x_mine + mine).astype(bf16)
        x_new = gather_from(x_mine, tensor, n_tensor, send_t).reshape(-1, width_local)
        rec_new = jnp.take(x_new, own_index, axis=0).reshape(rounds, rows_local, width_local)
        return x_new, rec_new, ext_new

    rows_all = gather_from(hidden, tensor, n_tensor, along_tensor(0))
    rows_all = rows_all.transpose(1, 0, 2, 3).reshape(-1, width_local)
    x = jnp.take(rows_all, sort_index, axis=0)
    record = None
    ext = None
    for step in range(n_segment):
        x_new, rec_new, ext_new = layer(x, step + 1 == n_segment, step)
        if step == 0:
            record, ext = rec_new, ext_new
        else:
            active = segment == step
            record = jnp.where(active, rec_new, record)
            ext = jnp.where(active, ext_new, ext)
        if step + 1 < n_segment:
            x = passed_along(x_new, "segment", 1)
    return (record[None], ext[None])


def solution(mesh):
    in_specs = (
        P(None, "tensor", "batch"),
        P("segment", "batch"),
        P("segment", "batch", "tensor"),
        P("segment", "batch", "tensor"),
        P("segment", "tensor", "batch"),
        P("segment", "batch", "tensor", None, None),
        P(),
        P(),
    )
    out_specs = (P("segment", None, "tensor", "batch"), P("segment", "batch", "tensor", None, None))
    return jax.shard_map(shards, mesh=mesh, in_specs=in_specs, out_specs=out_specs, check_vma=False)
```

```python
import jax
import jax.numpy as jnp
from jax import lax
from jax.sharding import PartitionSpec as P

MODEL_WIDTH = 16384
HEAD_SIZE = 128
DRAFT_BLOCK = 4
DECODE_ROUNDS = 3
GROUP_HEADS = 8


BATCH_INNER = 4


def shifted(x, axis, fn):
    n = lax.axis_size(axis)
    return lax.ppermute(x, axis, [(i, fn(i, n)) for i in range(n)])


def along_tensor(x, k):
    return shifted(x, "tensor", lambda i, n: (i + k) % n)


def along_y(x, k):
    return shifted(x, "by", lambda i, n: (i + k) % n)


def along_z(x, k):
    return shifted(x, "bz", lambda i, n: (i + k) % n)


def spread(blocks, pos, send):
    m = blocks.shape[0]
    out = [lax.dynamic_index_in_dim(blocks, pos, 0, keepdims=False)]
    for k in range(1, m):
        piece = lax.dynamic_index_in_dim(blocks, (pos + k) % m, 0, keepdims=False)
        out.append(send(piece, k))
    return out


def gather_from(x, pos, m, send):
    out = [x] + [send(x, k) for k in range(1, m)]
    order = (pos - jnp.arange(m)) % m
    return jnp.take(jnp.stack(out), order, axis=0)


def passed_along(block, axis, distance):
    devices = range(lax.axis_size(axis))
    route = [(i - distance, i) for i in devices if i - distance in devices]
    return lax.ppermute(block, axis, route)


def shards(
    hidden, norm_gain, w_query, key_value_weight, w_out, key_value_cache, owner_slot, accepted
):
    f32, bf16 = jnp.float32, jnp.bfloat16
    rounds, rows_local, width_local = hidden.shape
    n_segment = lax.axis_size("segment")
    segment = lax.axis_index("segment")
    tensor = lax.axis_index("tensor")
    group = lax.axis_index("bz") * lax.axis_size("by") + lax.axis_index("by")
    requests = owner_slot.shape[0]
    rows_total = requests * DRAFT_BLOCK
    slots_local = key_value_cache.shape[1]
    kv_local = key_value_cache.shape[2]
    query_cols = w_query.shape[2]
    kv_cols = key_value_weight.shape[2]
    block = rounds * DRAFT_BLOCK
    own_rows = slots_local * block
    req_local = rows_local // DRAFT_BLOCK
    scale = HEAD_SIZE ** (-0.5)
    gain = norm_gain[0].astype(f32)
    cache_local = key_value_cache[0]

    onehot = (owner_slot[None, :] == jnp.arange(requests)[:, None]).astype(jnp.int32)
    inverse = jnp.sum(onehot * jnp.arange(requests)[None, :], axis=1)
    acc_slot = jnp.sum(onehot[None] * accepted[:, None, :], axis=2)
    acc_own = lax.dynamic_slice_in_dim(acc_slot, group * slots_local, slots_local, 1)

    rr = jnp.arange(rounds)
    jj = jnp.arange(DRAFT_BLOCK)
    sort_index = (
        rr[None, :, None] * rows_total + inverse[:, None, None] * DRAFT_BLOCK + jj[None, None, :]
    ).reshape(-1)
    own_req = tensor * req_local + jnp.arange(req_local)
    own_index = (
        owner_slot[own_req][None, :, None] * block + rr[:, None, None] * DRAFT_BLOCK + jj[None, None, :]
    ).reshape(-1)

    pos = jnp.arange(block)
    r2 = pos // DRAFT_BLOCK
    place = pos % DRAFT_BLOCK
    acc_pos = acc_own[r2, :].T
    earlier = (r2[None, None, None, :] < rr[None, :, None, None]) & (
        place[None, None, None, :] < acc_pos[:, None, None, :]
    )
    same = (r2[None, :] == rr[:, None])[:, None, :] & (place[None, None, :] <= jj[None, :, None])
    valid = earlier | same[None]
    keep = place[None, :] < acc_pos

    n_tensor = lax.axis_size("tensor")
    n_y = BATCH_INNER
    n_z = lax.axis_size("bz")
    z_pos = group // n_y
    y_pos = group % n_y

    back_index = (
        owner_slot[None, :, None] * block + rr[:, None, None] * DRAFT_BLOCK + jj[None, None, :]
    ).reshape(-1)

    def layer(x_sorted, last):
        xf = x_sorted.astype(f32)
        sq = jnp.sum(xf * xf, axis=1, keepdims=True)
        sq_hi = sq.astype(bf16)
        sq_lo = (sq - sq_hi.astype(f32)).astype(bf16)
        xg = (xf * gain[None, :]).astype(bf16)
        first = jnp.dot(xg, w_query[0], preferred_element_type=f32)
        second = jnp.dot(xg, key_value_weight[0], preferred_element_type=f32)
        proj = jnp.concatenate([first.astype(bf16), second.astype(bf16), sq_hi, sq_lo], axis=1)
        cols = proj.shape[1]
        by_y = proj.reshape(n_z, n_y, own_rows, cols).transpose(1, 0, 2, 3)
        part = jnp.sum(lax.all_to_all(by_y, "by", 0, 0).astype(f32), axis=0)
        total = jnp.sum(lax.all_to_all(part, "bz", 0, 0), axis=0)
        total_sq = total[:, query_cols + kv_cols] + total[:, query_cols + kv_cols + 1]
        inv = lax.rsqrt(total_sq / MODEL_WIDTH + 1e-05)[:, None]
        query = (total[:, :query_cols] * inv).astype(bf16)
        keyval = (total[:, query_cols : query_cols + kv_cols] * inv).astype(bf16)
        query_heads = query.reshape(
            slots_local, rounds, DRAFT_BLOCK, kv_local, GROUP_HEADS, HEAD_SIZE
        )
        fresh = keyval.reshape(slots_local, block, kv_local, 2 * HEAD_SIZE).transpose(0, 2, 1, 3)
        s_cache = jnp.einsum(
            "srjhgd,shld->shgrjl", query_heads, cache_local[..., :HEAD_SIZE],
            preferred_element_type=f32,
        ) * scale
        s_fresh = jnp.einsum(
            "srjhgd,shld->shgrjl", query_heads, fresh[..., :HEAD_SIZE],
            preferred_element_type=f32,
        ) * scale
        s_fresh = jnp.where(valid[:, None, None], s_fresh, -1e30)
        scores = jnp.concatenate([s_cache, s_fresh], axis=-1)
        weights = jax.nn.softmax(scores, axis=-1).astype(bf16)
        values = jnp.concatenate([cache_local[..., HEAD_SIZE:], fresh[..., HEAD_SIZE:]], axis=2)
        attended = jnp.einsum(
            "shgrjl,shld->srjhgd", weights, values, preferred_element_type=f32
        )
        attended = attended.astype(bf16).reshape(own_rows, query_cols)
        by_z = gather_from(attended, z_pos, n_z, along_z)
        by_zy = gather_from(by_z, y_pos, n_y, along_y)
        gathered = by_zy.transpose(1, 0, 2, 3).reshape(-1, query_cols)
        partial = jnp.dot(gathered, w_out[0], preferred_element_type=f32)
        ext_new = jnp.where(keep[:, None, :, None], fresh, jnp.zeros_like(fresh))
        if last:
            natural = jnp.take(partial.astype(bf16), back_index, axis=0)
            pieces = natural.reshape(rounds, n_tensor, rows_local, width_local).transpose(1, 0, 2, 3)
            mine = jnp.sum(lax.all_to_all(pieces, "tensor", 0, 0).astype(f32), axis=0)
            x_own = jnp.take(xf, own_index, axis=0).reshape(rounds, rows_local, width_local)
            return None, (x_own + mine).astype(bf16), ext_new
        quarter = partial.shape[0] // n_tensor
        pieces = partial.astype(bf16).reshape(n_tensor, quarter, width_local)
        mine = jnp.sum(lax.all_to_all(pieces, "tensor", 0, 0).astype(f32), axis=0)
        x_mine = lax.dynamic_index_in_dim(
            xf.reshape(n_tensor, quarter, width_local), tensor, 0, keepdims=False
        )
        x_mine = (x_mine + mine).astype(bf16)
        x_new = gather_from(x_mine, tensor, n_tensor, along_tensor).reshape(-1, width_local)
        rec_new = jnp.take(x_new, own_index, axis=0).reshape(rounds, rows_local, width_local)
        return x_new, rec_new, ext_new

    rows_all = gather_from(hidden, tensor, n_tensor, along_tensor)
    rows_all = rows_all.transpose(1, 0, 2, 3).reshape(-1, width_local)
    x = jnp.take(rows_all, sort_index, axis=0)
    record = None
    ext = None
    for step in range(n_segment):
        x_new, rec_new, ext_new = layer(x, step + 1 == n_segment)
        if step == 0:
            record, ext = rec_new, ext_new
        else:
            active = segment == step
            record = jnp.where(active, rec_new, record)
            ext = jnp.where(active, ext_new, ext)
        if step + 1 < n_segment:
            x = passed_along(x_new, "segment", 1)
    return (record[None], ext[None])


def solution(mesh):
    n_batch = mesh.shape["batch"]
    inner = BATCH_INNER
    devices = mesh.devices.reshape(
        mesh.shape["segment"], mesh.shape["tensor"], n_batch // inner, inner
    )
    sub = jax.sharding.Mesh(devices, ("segment", "tensor", "bz", "by"))
    b = ("bz", "by")
    in_specs = (
        P(None, "tensor", b),
        P("segment", b),
        P("segment", b, "tensor"),
        P("segment", b, "tensor"),
        P("segment", "tensor", b),
        P("segment", b, "tensor", None, None),
        P(),
        P(),
    )
    out_specs = (P("segment", None, "tensor", b), P("segment", b, "tensor", None, None))
    return jax.shard_map(shards, mesh=sub, in_specs=in_specs, out_specs=out_specs, check_vma=False)
```

```python
import jax
import jax.numpy as jnp
from jax import lax
from jax.sharding import PartitionSpec as P

MODEL_WIDTH = 16384
HEAD_SIZE = 128
DRAFT_BLOCK = 4
DECODE_ROUNDS = 3
GROUP_HEADS = 8


BATCH_INNER = 4


def shifted(x, axis, fn):
    n = lax.axis_size(axis)
    return lax.ppermute(x, axis, [(i, fn(i, n)) for i in range(n)])


def along_tensor(x, k):
    return shifted(x, "tensor", lambda i, n: (i + k) % n)


def along_y(x, k):
    m = BATCH_INNER
    return shifted(x, "batch", lambda i, n: (i // m) * m + (i % m + k) % m)


def along_z(x, k):
    m = BATCH_INNER
    return shifted(x, "batch", lambda i, n: ((i // m + k) % (n // m)) * m + i % m)


def spread(blocks, pos, send):
    m = blocks.shape[0]
    out = [lax.dynamic_index_in_dim(blocks, pos, 0, keepdims=False)]
    for k in range(1, m):
        piece = lax.dynamic_index_in_dim(blocks, (pos + k) % m, 0, keepdims=False)
        out.append(send(piece, k))
    return out


def gather_from(x, pos, m, send):
    out = [x] + [send(x, k) for k in range(1, m)]
    order = (pos - jnp.arange(m)) % m
    return jnp.take(jnp.stack(out), order, axis=0)


def passed_along(block, axis, distance):
    devices = range(lax.axis_size(axis))
    route = [(i - distance, i) for i in devices if i - distance in devices]
    return lax.ppermute(block, axis, route)


def shards(
    hidden, norm_gain, w_query, key_value_weight, w_out, key_value_cache, owner_slot, accepted
):
    f32, bf16 = jnp.float32, jnp.bfloat16
    rounds, rows_local, width_local = hidden.shape
    n_segment = lax.axis_size("segment")
    segment = lax.axis_index("segment")
    tensor = lax.axis_index("tensor")
    group = lax.axis_index("batch")
    requests = owner_slot.shape[0]
    rows_total = requests * DRAFT_BLOCK
    slots_local = key_value_cache.shape[1]
    kv_local = key_value_cache.shape[2]
    query_cols = w_query.shape[2]
    kv_cols = key_value_weight.shape[2]
    block = rounds * DRAFT_BLOCK
    own_rows = slots_local * block
    req_local = rows_local // DRAFT_BLOCK
    scale = HEAD_SIZE ** (-0.5)
    gain = norm_gain[0].astype(f32)
    cache_local = key_value_cache[0]

    onehot = (owner_slot[None, :] == jnp.arange(requests)[:, None]).astype(jnp.int32)
    inverse = jnp.sum(onehot * jnp.arange(requests)[None, :], axis=1)
    acc_slot = jnp.sum(onehot[None] * accepted[:, None, :], axis=2)
    acc_own = lax.dynamic_slice_in_dim(acc_slot, group * slots_local, slots_local, 1)

    rr = jnp.arange(rounds)
    jj = jnp.arange(DRAFT_BLOCK)
    sort_index = (
        rr[None, :, None] * rows_total + inverse[:, None, None] * DRAFT_BLOCK + jj[None, None, :]
    ).reshape(-1)
    own_req = tensor * req_local + jnp.arange(req_local)
    own_index = (
        owner_slot[own_req][None, :, None] * block + rr[:, None, None] * DRAFT_BLOCK + jj[None, None, :]
    ).reshape(-1)

    pos = jnp.arange(block)
    r2 = pos // DRAFT_BLOCK
    place = pos % DRAFT_BLOCK
    acc_pos = acc_own[r2, :].T
    earlier = (r2[None, None, None, :] < rr[None, :, None, None]) & (
        place[None, None, None, :] < acc_pos[:, None, None, :]
    )
    same = (r2[None, :] == rr[:, None])[:, None, :] & (place[None, None, :] <= jj[None, :, None])
    valid = earlier | same[None]
    keep = place[None, :] < acc_pos

    n_tensor = lax.axis_size("tensor")
    n_y = BATCH_INNER
    n_z = lax.axis_size("batch") // n_y
    z_pos = group // n_y
    y_pos = group % n_y

    back_index = (
        owner_slot[None, :, None] * block + rr[:, None, None] * DRAFT_BLOCK + jj[None, None, :]
    ).reshape(-1)

    def layer(x_sorted, last):
        xf = x_sorted.astype(f32)
        sq = jnp.sum(xf * xf, axis=1, keepdims=True)
        sq_hi = sq.astype(bf16)
        sq_lo = (sq - sq_hi.astype(f32)).astype(bf16)
        xg = (xf * gain[None, :]).astype(bf16)
        first = jnp.dot(xg, w_query[0], preferred_element_type=f32)
        second = jnp.dot(xg, key_value_weight[0], preferred_element_type=f32)
        proj = jnp.concatenate([first.astype(bf16), second.astype(bf16), sq_hi, sq_lo], axis=1)
        cols = proj.shape[1]
        blocks = proj.reshape(n_z, n_y, own_rows, cols)
        cut = (cols // 2) // 128 * 128
        first_y = blocks[..., :cut].transpose(1, 0, 2, 3)
        first_z = blocks[..., cut:]
        part_a = sum(r.astype(f32) for r in spread(first_y, y_pos, along_y))
        part_b = sum(r.astype(f32) for r in spread(first_z, z_pos, along_z))
        total_a = sum(spread(part_a, z_pos, along_z))
        total_b = sum(spread(part_b, y_pos, along_y))
        total = jnp.concatenate([total_a, total_b], axis=1)
        total_sq = total[:, query_cols + kv_cols] + total[:, query_cols + kv_cols + 1]
        inv = lax.rsqrt(total_sq / MODEL_WIDTH + 1e-05)[:, None]
        query = (total[:, :query_cols] * inv).astype(bf16)
        keyval = (total[:, query_cols : query_cols + kv_cols] * inv).astype(bf16)
        query_heads = query.reshape(
            slots_local, rounds, DRAFT_BLOCK, kv_local, GROUP_HEADS, HEAD_SIZE
        )
        fresh = keyval.reshape(slots_local, block, kv_local, 2 * HEAD_SIZE).transpose(0, 2, 1, 3)
        s_cache = jnp.einsum(
            "srjhgd,shld->shgrjl", query_heads, cache_local[..., :HEAD_SIZE],
            preferred_element_type=f32,
        ) * scale
        s_fresh = jnp.einsum(
            "srjhgd,shld->shgrjl", query_heads, fresh[..., :HEAD_SIZE],
            preferred_element_type=f32,
        ) * scale
        s_fresh = jnp.where(valid[:, None, None], s_fresh, -1e30)
        scores = jnp.concatenate([s_cache, s_fresh], axis=-1)
        weights = jax.nn.softmax(scores, axis=-1).astype(bf16)
        values = jnp.concatenate([cache_local[..., HEAD_SIZE:], fresh[..., HEAD_SIZE:]], axis=2)
        attended = jnp.einsum(
            "shgrjl,shld->srjhgd", weights, values, preferred_element_type=f32
        )
        attended = attended.astype(bf16).reshape(own_rows, query_cols)
        split = query_cols // 2
        via_z = gather_from(attended[:, :split], z_pos, n_z, along_z)
        via_z = gather_from(via_z, y_pos, n_y, along_y).transpose(1, 0, 2, 3).reshape(-1, split)
        via_y = gather_from(attended[:, split:], y_pos, n_y, along_y)
        via_y = gather_from(via_y, z_pos, n_z, along_z).reshape(-1, query_cols - split)
        partial = jnp.dot(via_z, w_out[0, :split], preferred_element_type=f32) + jnp.dot(
            via_y, w_out[0, split:], preferred_element_type=f32
        )
        ext_new = jnp.where(keep[:, None, :, None], fresh, jnp.zeros_like(fresh))
        if last:
            natural = jnp.take(partial.astype(bf16), back_index, axis=0)
            pieces = natural.reshape(rounds, n_tensor, rows_local, width_local).transpose(1, 0, 2, 3)
            mine = sum(r.astype(f32) for r in spread(pieces, tensor, along_tensor))
            x_own = jnp.take(xf, own_index, axis=0).reshape(rounds, rows_local, width_local)
            return None, (x_own + mine).astype(bf16), ext_new
        quarter = partial.shape[0] // n_tensor
        pieces = partial.astype(bf16).reshape(n_tensor, quarter, width_local)
        mine = sum(r.astype(f32) for r in spread(pieces, tensor, along_tensor))
        x_mine = lax.dynamic_index_in_dim(
            xf.reshape(n_tensor, quarter, width_local), tensor, 0, keepdims=False
        )
        x_mine = (x_mine + mine).astype(bf16)
        x_new = gather_from(x_mine, tensor, n_tensor, along_tensor).reshape(-1, width_local)
        rec_new = jnp.take(x_new, own_index, axis=0).reshape(rounds, rows_local, width_local)
        return x_new, rec_new, ext_new

    rows_all = gather_from(hidden, tensor, n_tensor, along_tensor)
    rows_all = rows_all.transpose(1, 0, 2, 3).reshape(-1, width_local)
    x = jnp.take(rows_all, sort_index, axis=0)
    record = None
    ext = None
    for step in range(n_segment):
        x_new, rec_new, ext_new = layer(x, step + 1 == n_segment)
        if step == 0:
            record, ext = rec_new, ext_new
        else:
            active = segment == step
            record = jnp.where(active, rec_new, record)
            ext = jnp.where(active, ext_new, ext)
        if step + 1 < n_segment:
            x = passed_along(x_new, "segment", 1)
    return (record[None], ext[None])


def solution(mesh):
    in_specs = (
        P(None, "tensor", "batch"),
        P("segment", "batch"),
        P("segment", "batch", "tensor"),
        P("segment", "batch", "tensor"),
        P("segment", "tensor", "batch"),
        P("segment", "batch", "tensor", None, None),
        P(),
        P(),
    )
    out_specs = (P("segment", None, "tensor", "batch"), P("segment", "batch", "tensor", None, None))
    return jax.shard_map(shards, mesh=mesh, in_specs=in_specs, out_specs=out_specs, check_vma=False)
```

```python
import jax
import jax.numpy as jnp
from jax import lax
from jax.sharding import PartitionSpec as P

MODEL_WIDTH = 16384
HEAD_SIZE = 128
DRAFT_BLOCK = 4
DECODE_ROUNDS = 3
GROUP_HEADS = 8


BATCH_INNER = 4


def shifted(x, axis, fn):
    n = lax.axis_size(axis)
    return lax.ppermute(x, axis, [(i, fn(i, n)) for i in range(n)])


def along_tensor(x, k):
    return shifted(x, "tensor", lambda i, n: (i + k) % n)


def along_y(x, k):
    m = BATCH_INNER
    return shifted(x, "batch", lambda i, n: (i // m) * m + (i % m + k) % m)


def along_z(x, k):
    m = BATCH_INNER
    return shifted(x, "batch", lambda i, n: ((i // m + k) % (n // m)) * m + i % m)


def spread(blocks, pos, send):
    m = blocks.shape[0]
    out = [lax.dynamic_index_in_dim(blocks, pos, 0, keepdims=False)]
    for k in range(1, m):
        piece = lax.dynamic_index_in_dim(blocks, (pos + k) % m, 0, keepdims=False)
        out.append(send(piece, k))
    return out


def gather_from(x, pos, m, send):
    out = [x] + [send(x, k) for k in range(1, m)]
    order = (pos - jnp.arange(m)) % m
    return jnp.take(jnp.stack(out), order, axis=0)


def passed_along(block, axis, distance):
    devices = range(lax.axis_size(axis))
    route = [(i - distance, i) for i in devices if i - distance in devices]
    return lax.ppermute(block, axis, route)


def handed_on(x, step, pos):
    n = lax.axis_size("tensor")
    outs = []
    for k in range(n):
        pairs = [(step * n + t, (step + 1) * n + (t + k) % n) for t in range(n)]
        outs.append(lax.ppermute(x, ("segment", "tensor"), pairs))
    order = (pos - jnp.arange(n)) % n
    return jnp.take(jnp.stack(outs), order, axis=0)


def shards(
    hidden, norm_gain, w_query, key_value_weight, w_out, key_value_cache, owner_slot, accepted
):
    f32, bf16 = jnp.float32, jnp.bfloat16
    rounds, rows_local, width_local = hidden.shape
    n_segment = lax.axis_size("segment")
    segment = lax.axis_index("segment")
    tensor = lax.axis_index("tensor")
    group = lax.axis_index("batch")
    requests = owner_slot.shape[0]
    rows_total = requests * DRAFT_BLOCK
    slots_local = key_value_cache.shape[1]
    kv_local = key_value_cache.shape[2]
    query_cols = w_query.shape[2]
    kv_cols = key_value_weight.shape[2]
    block = rounds * DRAFT_BLOCK
    own_rows = slots_local * block
    req_local = rows_local // DRAFT_BLOCK
    scale = HEAD_SIZE ** (-0.5)
    gain = norm_gain[0].astype(f32)
    cache_local = key_value_cache[0]

    onehot = (owner_slot[None, :] == jnp.arange(requests)[:, None]).astype(jnp.int32)
    inverse = jnp.sum(onehot * jnp.arange(requests)[None, :], axis=1)
    acc_slot = jnp.sum(onehot[None] * accepted[:, None, :], axis=2)
    acc_own = lax.dynamic_slice_in_dim(acc_slot, group * slots_local, slots_local, 1)

    rr = jnp.arange(rounds)
    jj = jnp.arange(DRAFT_BLOCK)
    sort_index = (
        rr[None, :, None] * rows_total + inverse[:, None, None] * DRAFT_BLOCK + jj[None, None, :]
    ).reshape(-1)
    own_req = tensor * req_local + jnp.arange(req_local)
    own_index = (
        owner_slot[own_req][None, :, None] * block + rr[:, None, None] * DRAFT_BLOCK + jj[None, None, :]
    ).reshape(-1)

    pos = jnp.arange(block)
    r2 = pos // DRAFT_BLOCK
    place = pos % DRAFT_BLOCK
    acc_pos = acc_own[r2, :].T
    earlier = (r2[None, None, None, :] < rr[None, :, None, None]) & (
        place[None, None, None, :] < acc_pos[:, None, None, :]
    )
    same = (r2[None, :] == rr[:, None])[:, None, :] & (place[None, None, :] <= jj[None, :, None])
    valid = earlier | same[None]
    keep = place[None, :] < acc_pos

    n_tensor = lax.axis_size("tensor")
    n_y = BATCH_INNER
    n_z = lax.axis_size("batch") // n_y
    z_pos = group // n_y
    y_pos = group % n_y

    back_index = (
        owner_slot[None, :, None] * block + rr[:, None, None] * DRAFT_BLOCK + jj[None, None, :]
    ).reshape(-1)

    def layer(x_sorted):
        xf = x_sorted.astype(f32)
        sq = jnp.sum(xf * xf, axis=1, keepdims=True)
        sq_hi = sq.astype(bf16)
        sq_lo = (sq - sq_hi.astype(f32)).astype(bf16)
        xg = (xf * gain[None, :]).astype(bf16)
        first = jnp.dot(xg, w_query[0], preferred_element_type=f32)
        second = jnp.dot(xg, key_value_weight[0], preferred_element_type=f32)
        proj = jnp.concatenate([first.astype(bf16), second.astype(bf16), sq_hi, sq_lo], axis=1)
        cols = proj.shape[1]
        blocks = proj.reshape(n_z, n_y, own_rows, cols)
        cut = (cols // 2) // 128 * 128
        first_y = blocks[..., :cut].transpose(1, 0, 2, 3)
        first_z = blocks[..., cut:]
        part_a = sum(r.astype(f32) for r in spread(first_y, y_pos, along_y))
        part_b = sum(r.astype(f32) for r in spread(first_z, z_pos, along_z))
        total_a = sum(spread(part_a, z_pos, along_z))
        total_b = sum(spread(part_b, y_pos, along_y))
        total = jnp.concatenate([total_a, total_b], axis=1)
        total_sq = total[:, query_cols + kv_cols] + total[:, query_cols + kv_cols + 1]
        inv = lax.rsqrt(total_sq / MODEL_WIDTH + 1e-05)[:, None]
        query = (total[:, :query_cols] * inv).astype(bf16)
        keyval = (total[:, query_cols : query_cols + kv_cols] * inv).astype(bf16)
        query_heads = query.reshape(
            slots_local, rounds, DRAFT_BLOCK, kv_local, GROUP_HEADS, HEAD_SIZE
        )
        fresh = keyval.reshape(slots_local, block, kv_local, 2 * HEAD_SIZE).transpose(0, 2, 1, 3)
        s_cache = jnp.einsum(
            "srjhgd,shld->shgrjl", query_heads, cache_local[..., :HEAD_SIZE],
            preferred_element_type=f32,
        ) * scale
        s_fresh = jnp.einsum(
            "srjhgd,shld->shgrjl", query_heads, fresh[..., :HEAD_SIZE],
            preferred_element_type=f32,
        ) * scale
        s_fresh = jnp.where(valid[:, None, None], s_fresh, -1e30)
        scores = jnp.concatenate([s_cache, s_fresh], axis=-1)
        weights = jax.nn.softmax(scores, axis=-1).astype(bf16)
        values = jnp.concatenate([cache_local[..., HEAD_SIZE:], fresh[..., HEAD_SIZE:]], axis=2)
        attended = jnp.einsum(
            "shgrjl,shld->srjhgd", weights, values, preferred_element_type=f32
        )
        attended = attended.astype(bf16).reshape(own_rows, query_cols)
        split = query_cols // 2
        via_z = gather_from(attended[:, :split], z_pos, n_z, along_z)
        via_z = gather_from(via_z, y_pos, n_y, along_y).transpose(1, 0, 2, 3).reshape(-1, split)
        via_y = gather_from(attended[:, split:], y_pos, n_y, along_y)
        via_y = gather_from(via_y, z_pos, n_z, along_z).reshape(-1, query_cols - split)
        partial = jnp.dot(via_z, w_out[0, :split], preferred_element_type=f32) + jnp.dot(
            via_y, w_out[0, split:], preferred_element_type=f32
        )
        ext_new = jnp.where(keep[:, None, :, None], fresh, jnp.zeros_like(fresh))
        natural = jnp.take(partial.astype(bf16), back_index, axis=0)
        pieces = natural.reshape(rounds, n_tensor, rows_local, width_local).transpose(1, 0, 2, 3)
        mine = sum(r.astype(f32) for r in spread(pieces, tensor, along_tensor))
        x_own = jnp.take(xf, own_index, axis=0).reshape(rounds, rows_local, width_local)
        return (x_own + mine).astype(bf16), ext_new

    rows = gather_from(hidden, tensor, n_tensor, along_tensor)
    record = None
    ext = None
    for step in range(n_segment):
        rows_all = rows.transpose(1, 0, 2, 3).reshape(-1, width_local)
        rec_new, ext_new = layer(jnp.take(rows_all, sort_index, axis=0))
        if step == 0:
            record, ext = rec_new, ext_new
        else:
            active = segment == step
            record = jnp.where(active, rec_new, record)
            ext = jnp.where(active, ext_new, ext)
        if step + 1 < n_segment:
            rows = handed_on(rec_new, step, tensor)
    return (record[None], ext[None])


def solution(mesh):
    in_specs = (
        P(None, "tensor", "batch"),
        P("segment", "batch"),
        P("segment", "batch", "tensor"),
        P("segment", "batch", "tensor"),
        P("segment", "tensor", "batch"),
        P("segment", "batch", "tensor", None, None),
        P(),
        P(),
    )
    out_specs = (P("segment", None, "tensor", "batch"), P("segment", "batch", "tensor", None, None))
    return jax.shard_map(shards, mesh=mesh, in_specs=in_specs, out_specs=out_specs, check_vma=False)
```

```python
import jax
import jax.numpy as jnp
from jax import lax
from jax.sharding import PartitionSpec as P

MODEL_WIDTH = 16384
HEAD_SIZE = 128
DRAFT_BLOCK = 4
DECODE_ROUNDS = 3
GROUP_HEADS = 8


BATCH_INNER = 4


def shifted(x, axis, fn):
    n = lax.axis_size(axis)
    return lax.ppermute(x, axis, [(i, fn(i, n)) for i in range(n)])


def along_tensor(x, k):
    return shifted(x, "tensor", lambda i, n: (i + k) % n)


def along_y(x, k):
    m = BATCH_INNER
    return shifted(x, "batch", lambda i, n: (i // m) * m + (i % m + k) % m)


def along_z(x, k):
    m = BATCH_INNER
    return shifted(x, "batch", lambda i, n: ((i // m + k) % (n // m)) * m + i % m)


def spread(blocks, pos, send):
    m = blocks.shape[0]
    out = [lax.dynamic_index_in_dim(blocks, pos, 0, keepdims=False)]
    for k in range(1, m):
        piece = lax.dynamic_index_in_dim(blocks, (pos + k) % m, 0, keepdims=False)
        out.append(send(piece, k))
    return out


def gather_from(x, pos, m, send):
    out = [x] + [send(x, k) for k in range(1, m)]
    order = (pos - jnp.arange(m)) % m
    return jnp.take(jnp.stack(out), order, axis=0)


def passed_along(block, axis, distance):
    devices = range(lax.axis_size(axis))
    route = [(i - distance, i) for i in devices if i - distance in devices]
    return lax.ppermute(block, axis, route)


def reduce_over(blocks, axis):
    return jnp.sum(lax.all_to_all(blocks, axis, 0, 0).astype(jnp.float32), axis=0)


def gather_over(x, axis):
    m = lax.axis_size(axis)
    return lax.all_to_all(jnp.broadcast_to(x[None], (m,) + x.shape), axis, 0, 0)


def handed_on(x, step, pos):
    n = lax.axis_size("tensor")
    outs = []
    for k in range(n):
        pairs = [(step * n + t, (step + 1) * n + (t + k) % n) for t in range(n)]
        outs.append(lax.ppermute(x, ("segment", "tensor"), pairs))
    order = (pos - jnp.arange(n)) % n
    return jnp.take(jnp.stack(outs), order, axis=0)


def shards(
    hidden, norm_gain, w_query, key_value_weight, w_out, key_value_cache, owner_slot, accepted
):
    f32, bf16 = jnp.float32, jnp.bfloat16
    rounds, rows_local, width_local = hidden.shape
    n_segment = lax.axis_size("segment")
    segment = lax.axis_index("segment")
    tensor = lax.axis_index("tensor")
    group = lax.axis_index("bz") * lax.axis_size("by") + lax.axis_index("by")
    requests = owner_slot.shape[0]
    rows_total = requests * DRAFT_BLOCK
    slots_local = key_value_cache.shape[1]
    kv_local = key_value_cache.shape[2]
    query_cols = w_query.shape[2]
    kv_cols = key_value_weight.shape[2]
    block = rounds * DRAFT_BLOCK
    own_rows = slots_local * block
    req_local = rows_local // DRAFT_BLOCK
    scale = HEAD_SIZE ** (-0.5)
    gain = norm_gain[0].astype(f32)
    cache_local = key_value_cache[0]

    onehot = (owner_slot[None, :] == jnp.arange(requests)[:, None]).astype(jnp.int32)
    inverse = jnp.sum(onehot * jnp.arange(requests)[None, :], axis=1)
    acc_slot = jnp.sum(onehot[None] * accepted[:, None, :], axis=2)
    acc_own = lax.dynamic_slice_in_dim(acc_slot, group * slots_local, slots_local, 1)

    rr = jnp.arange(rounds)
    jj = jnp.arange(DRAFT_BLOCK)
    sort_index = (
        rr[None, :, None] * rows_total + inverse[:, None, None] * DRAFT_BLOCK + jj[None, None, :]
    ).reshape(-1)
    own_req = tensor * req_local + jnp.arange(req_local)
    own_index = (
        owner_slot[own_req][None, :, None] * block + rr[:, None, None] * DRAFT_BLOCK + jj[None, None, :]
    ).reshape(-1)

    pos = jnp.arange(block)
    r2 = pos // DRAFT_BLOCK
    place = pos % DRAFT_BLOCK
    acc_pos = acc_own[r2, :].T
    earlier = (r2[None, None, None, :] < rr[None, :, None, None]) & (
        place[None, None, None, :] < acc_pos[:, None, None, :]
    )
    same = (r2[None, :] == rr[:, None])[:, None, :] & (place[None, None, :] <= jj[None, :, None])
    valid = earlier | same[None]
    keep = place[None, :] < acc_pos

    n_tensor = lax.axis_size("tensor")
    n_y = BATCH_INNER
    n_z = lax.axis_size("bz")
    z_pos = group // n_y
    y_pos = group % n_y

    back_index = (
        owner_slot[None, :, None] * block + rr[:, None, None] * DRAFT_BLOCK + jj[None, None, :]
    ).reshape(-1)

    def layer(x_sorted):
        xf = x_sorted.astype(f32)
        sq = jnp.sum(xf * xf, axis=1, keepdims=True)
        sq_hi = sq.astype(bf16)
        sq_lo = (sq - sq_hi.astype(f32)).astype(bf16)
        xg = (xf * gain[None, :]).astype(bf16)
        first = jnp.dot(xg, w_query[0], preferred_element_type=f32)
        second = jnp.dot(xg, key_value_weight[0], preferred_element_type=f32)
        proj = jnp.concatenate([first.astype(bf16), second.astype(bf16), sq_hi, sq_lo], axis=1)
        cols = proj.shape[1]
        blocks = proj.reshape(n_z, n_y, own_rows, cols)
        cut = (cols // 2) // 128 * 128
        first_y = blocks[..., :cut].transpose(1, 0, 2, 3)
        first_z = blocks[..., cut:]
        part_a = reduce_over(first_y, "by")
        part_b = reduce_over(first_z, "bz")
        total_a = reduce_over(part_a, "bz")
        total_b = reduce_over(part_b, "by")
        total = jnp.concatenate([total_a, total_b], axis=1)
        total_sq = total[:, query_cols + kv_cols] + total[:, query_cols + kv_cols + 1]
        inv = lax.rsqrt(total_sq / MODEL_WIDTH + 1e-05)[:, None]
        query = (total[:, :query_cols] * inv).astype(bf16)
        keyval = (total[:, query_cols : query_cols + kv_cols] * inv).astype(bf16)
        query_heads = query.reshape(
            slots_local, rounds, DRAFT_BLOCK, kv_local, GROUP_HEADS, HEAD_SIZE
        )
        fresh = keyval.reshape(slots_local, block, kv_local, 2 * HEAD_SIZE).transpose(0, 2, 1, 3)
        s_cache = jnp.einsum(
            "srjhgd,shld->shgrjl", query_heads, cache_local[..., :HEAD_SIZE],
            preferred_element_type=f32,
        ) * scale
        s_fresh = jnp.einsum(
            "srjhgd,shld->shgrjl", query_heads, fresh[..., :HEAD_SIZE],
            preferred_element_type=f32,
        ) * scale
        s_fresh = jnp.where(valid[:, None, None], s_fresh, -1e30)
        scores = jnp.concatenate([s_cache, s_fresh], axis=-1)
        weights = jax.nn.softmax(scores, axis=-1).astype(bf16)
        values = jnp.concatenate([cache_local[..., HEAD_SIZE:], fresh[..., HEAD_SIZE:]], axis=2)
        attended = jnp.einsum(
            "shgrjl,shld->srjhgd", weights, values, preferred_element_type=f32
        )
        attended = attended.astype(bf16).reshape(own_rows, query_cols)
        split = query_cols // 2
        via_z = gather_over(attended[:, :split], "bz")
        via_z = gather_over(via_z, "by").transpose(1, 0, 2, 3).reshape(-1, split)
        via_y = gather_over(attended[:, split:], "by")
        via_y = gather_over(via_y, "bz").reshape(-1, query_cols - split)
        partial = jnp.dot(via_z, w_out[0, :split], preferred_element_type=f32) + jnp.dot(
            via_y, w_out[0, split:], preferred_element_type=f32
        )
        ext_new = jnp.where(keep[:, None, :, None], fresh, jnp.zeros_like(fresh))
        natural = jnp.take(partial.astype(bf16), back_index, axis=0)
        pieces = natural.reshape(rounds, n_tensor, rows_local, width_local).transpose(1, 0, 2, 3)
        mine = reduce_over(pieces, "tensor")
        x_own = jnp.take(xf, own_index, axis=0).reshape(rounds, rows_local, width_local)
        return (x_own + mine).astype(bf16), ext_new

    rows = gather_over(hidden, "tensor")
    record = None
    ext = None
    for step in range(n_segment):
        rows_all = rows.transpose(1, 0, 2, 3).reshape(-1, width_local)
        rec_new, ext_new = layer(jnp.take(rows_all, sort_index, axis=0))
        if step == 0:
            record, ext = rec_new, ext_new
        else:
            active = segment == step
            record = jnp.where(active, rec_new, record)
            ext = jnp.where(active, ext_new, ext)
        if step + 1 < n_segment:
            rows = handed_on(rec_new, step, tensor)
    return (record[None], ext[None])


def solution(mesh):
    n_batch = mesh.shape["batch"]
    inner = BATCH_INNER
    devices = mesh.devices.reshape(
        mesh.shape["segment"], mesh.shape["tensor"], n_batch // inner, inner
    )
    sub = jax.sharding.Mesh(devices, ("segment", "tensor", "bz", "by"))
    b = ("bz", "by")
    in_specs = (
        P(None, "tensor", b),
        P("segment", b),
        P("segment", b, "tensor"),
        P("segment", b, "tensor"),
        P("segment", "tensor", b),
        P("segment", b, "tensor", None, None),
        P(),
        P(),
    )
    out_specs = (P("segment", None, "tensor", b), P("segment", b, "tensor", None, None))
    return jax.shard_map(shards, mesh=sub, in_specs=in_specs, out_specs=out_specs, check_vma=False)
```

```python
import jax
import jax.numpy as jnp
from jax import lax
from jax.sharding import PartitionSpec as P

MODEL_WIDTH = 16384
HEAD_SIZE = 128
DRAFT_BLOCK = 4
DECODE_ROUNDS = 3
GROUP_HEADS = 8


BATCH_INNER = 4


def shifted(x, axis, fn):
    n = lax.axis_size(axis)
    return lax.ppermute(x, axis, [(i, fn(i, n)) for i in range(n)])


def along_tensor(x, k):
    return shifted(x, "tensor", lambda i, n: (i + k) % n)


def along_y(x, k):
    m = BATCH_INNER
    return shifted(x, "batch", lambda i, n: (i // m) * m + (i % m + k) % m)


def along_z(x, k):
    m = BATCH_INNER
    return shifted(x, "batch", lambda i, n: ((i // m + k) % (n // m)) * m + i % m)


def spread(blocks, pos, send):
    m = blocks.shape[0]
    out = [lax.dynamic_index_in_dim(blocks, pos, 0, keepdims=False)]
    for k in range(1, m):
        piece = lax.dynamic_index_in_dim(blocks, (pos + k) % m, 0, keepdims=False)
        out.append(send(piece, k))
    return out


def gather_from(x, pos, m, send):
    out = [x] + [send(x, k) for k in range(1, m)]
    order = (pos - jnp.arange(m)) % m
    return jnp.take(jnp.stack(out), order, axis=0)


def passed_along(block, axis, distance):
    devices = range(lax.axis_size(axis))
    route = [(i - distance, i) for i in devices if i - distance in devices]
    return lax.ppermute(block, axis, route)


def shards(
    hidden, norm_gain, w_query, key_value_weight, w_out, key_value_cache, owner_slot, accepted
):
    f32, bf16 = jnp.float32, jnp.bfloat16
    rounds, rows_local, width_local = hidden.shape
    n_segment = lax.axis_size("segment")
    segment = lax.axis_index("segment")
    tensor = lax.axis_index("tensor")
    group = lax.axis_index("batch")
    requests = owner_slot.shape[0]
    rows_total = requests * DRAFT_BLOCK
    slots_local = key_value_cache.shape[1]
    kv_local = key_value_cache.shape[2]
    query_cols = w_query.shape[2]
    kv_cols = key_value_weight.shape[2]
    block = rounds * DRAFT_BLOCK
    own_rows = slots_local * block
    req_local = rows_local // DRAFT_BLOCK
    scale = HEAD_SIZE ** (-0.5)
    gain = norm_gain[0].astype(f32)
    cache_local = key_value_cache[0]

    onehot = (owner_slot[None, :] == jnp.arange(requests)[:, None]).astype(jnp.int32)
    inverse = jnp.sum(onehot * jnp.arange(requests)[None, :], axis=1)
    acc_slot = jnp.sum(onehot[None] * accepted[:, None, :], axis=2)
    acc_own = lax.dynamic_slice_in_dim(acc_slot, group * slots_local, slots_local, 1)

    rr = jnp.arange(rounds)
    jj = jnp.arange(DRAFT_BLOCK)
    sort_index = (
        rr[None, :, None] * rows_total + inverse[:, None, None] * DRAFT_BLOCK + jj[None, None, :]
    ).reshape(-1)
    own_req = tensor * req_local + jnp.arange(req_local)
    own_index = (
        owner_slot[own_req][None, :, None] * block + rr[:, None, None] * DRAFT_BLOCK + jj[None, None, :]
    ).reshape(-1)

    pos = jnp.arange(block)
    r2 = pos // DRAFT_BLOCK
    place = pos % DRAFT_BLOCK
    acc_pos = acc_own[r2, :].T
    earlier = (r2[None, None, None, :] < rr[None, :, None, None]) & (
        place[None, None, None, :] < acc_pos[:, None, None, :]
    )
    same = (r2[None, :] == rr[:, None])[:, None, :] & (place[None, None, :] <= jj[None, :, None])
    valid = earlier | same[None]
    keep = place[None, :] < acc_pos

    n_tensor = lax.axis_size("tensor")
    n_y = BATCH_INNER
    n_z = lax.axis_size("batch") // n_y
    z_pos = group // n_y
    y_pos = group % n_y

    back_index = (
        owner_slot[None, :, None] * block + rr[:, None, None] * DRAFT_BLOCK + jj[None, None, :]
    ).reshape(-1)

    def layer(x_sorted, last):
        xf = x_sorted.astype(f32)
        sq = jnp.sum(xf * xf, axis=1, keepdims=True)
        sq_hi = sq.astype(bf16)
        sq_lo = (sq - sq_hi.astype(f32)).astype(bf16)
        xg = (xf * gain[None, :]).astype(bf16)
        first = jnp.dot(xg, w_query[0], preferred_element_type=f32)
        second = jnp.dot(xg, key_value_weight[0], preferred_element_type=f32)
        proj = jnp.concatenate([first.astype(bf16), second.astype(bf16), sq_hi, sq_lo], axis=1)
        cols = proj.shape[1]
        blocks = proj.reshape(n_z, n_y, own_rows, cols)
        cut = (cols // 2) // 128 * 128
        first_y = blocks[..., :cut].transpose(1, 0, 2, 3)
        first_z = blocks[..., cut:]
        part_a = sum(r.astype(f32) for r in spread(first_y, y_pos, along_y))
        part_b = sum(r.astype(f32) for r in spread(first_z, z_pos, along_z))
        total_a = sum(spread(part_a, z_pos, along_z))
        total_b = sum(spread(part_b, y_pos, along_y))
        total = jnp.concatenate([total_a, total_b], axis=1)
        total_sq = total[:, query_cols + kv_cols] + total[:, query_cols + kv_cols + 1]
        inv = lax.rsqrt(total_sq / MODEL_WIDTH + 1e-05)[:, None]
        query = (total[:, :query_cols] * inv).astype(bf16)
        keyval = (total[:, query_cols : query_cols + kv_cols] * inv).astype(bf16)
        query_heads = query.reshape(
            slots_local, rounds, DRAFT_BLOCK, kv_local, GROUP_HEADS, HEAD_SIZE
        )
        fresh = keyval.reshape(slots_local, block, kv_local, 2 * HEAD_SIZE).transpose(0, 2, 1, 3)
        s_cache = jnp.einsum(
            "srjhgd,shld->shgrjl", query_heads, cache_local[..., :HEAD_SIZE],
            preferred_element_type=f32,
        ) * scale
        s_fresh = jnp.einsum(
            "srjhgd,shld->shgrjl", query_heads, fresh[..., :HEAD_SIZE],
            preferred_element_type=f32,
        ) * scale
        s_fresh = jnp.where(valid[:, None, None], s_fresh, -1e30)
        scores = jnp.concatenate([s_cache, s_fresh], axis=-1)
        weights = jax.nn.softmax(scores, axis=-1).astype(bf16)
        values = jnp.concatenate([cache_local[..., HEAD_SIZE:], fresh[..., HEAD_SIZE:]], axis=2)
        attended = jnp.einsum(
            "shgrjl,shld->srjhgd", weights, values, preferred_element_type=f32
        )
        attended = attended.astype(bf16).reshape(own_rows, query_cols)
        by_z = gather_from(attended, z_pos, n_z, along_z)
        by_zy = gather_from(by_z, y_pos, n_y, along_y)
        gathered = by_zy.transpose(1, 0, 2, 3).reshape(-1, query_cols)
        partial = jnp.dot(gathered, w_out[0], preferred_element_type=f32)
        ext_new = jnp.where(keep[:, None, :, None], fresh, jnp.zeros_like(fresh))
        if last:
            natural = jnp.take(partial.astype(bf16), back_index, axis=0)
            pieces = natural.reshape(rounds, n_tensor, rows_local, width_local).transpose(1, 0, 2, 3)
            mine = sum(r.astype(f32) for r in spread(pieces, tensor, along_tensor))
            x_own = jnp.take(xf, own_index, axis=0).reshape(rounds, rows_local, width_local)
            return None, (x_own + mine).astype(bf16), ext_new
        quarter = partial.shape[0] // n_tensor
        pieces = partial.astype(bf16).reshape(n_tensor, quarter, width_local)
        mine = sum(r.astype(f32) for r in spread(pieces, tensor, along_tensor))
        x_mine = lax.dynamic_index_in_dim(
            xf.reshape(n_tensor, quarter, width_local), tensor, 0, keepdims=False
        )
        x_mine = (x_mine + mine).astype(bf16)
        x_new = gather_from(x_mine, tensor, n_tensor, along_tensor).reshape(-1, width_local)
        rec_new = jnp.take(x_new, own_index, axis=0).reshape(rounds, rows_local, width_local)
        return x_new, rec_new, ext_new

    rows_all = gather_from(hidden, tensor, n_tensor, along_tensor)
    rows_all = rows_all.transpose(1, 0, 2, 3).reshape(-1, width_local)
    x = jnp.take(rows_all, sort_index, axis=0)
    record = None
    ext = None
    for step in range(n_segment):
        x_new, rec_new, ext_new = layer(x, step + 1 == n_segment)
        if step == 0:
            record, ext = rec_new, ext_new
        else:
            active = segment == step
            record = jnp.where(active, rec_new, record)
            ext = jnp.where(active, ext_new, ext)
        if step + 1 < n_segment:
            x = passed_along(x_new, "segment", 1)
    return (record[None], ext[None])


def solution(mesh):
    in_specs = (
        P(None, "tensor", "batch"),
        P("segment", "batch"),
        P("segment", "batch", "tensor"),
        P("segment", "batch", "tensor"),
        P("segment", "tensor", "batch"),
        P("segment", "batch", "tensor", None, None),
        P(),
        P(),
    )
    out_specs = (P("segment", None, "tensor", "batch"), P("segment", "batch", "tensor", None, None))
    return jax.shard_map(shards, mesh=mesh, in_specs=in_specs, out_specs=out_specs, check_vma=False)
```

```python
import jax
import jax.numpy as jnp
from jax import lax
from jax.sharding import PartitionSpec as P

MODEL_WIDTH = 16384
HEAD_SIZE = 128
DRAFT_BLOCK = 4
DECODE_ROUNDS = 3
GROUP_HEADS = 8


BATCH_INNER = 4


def shifted(x, axis, fn):
    n = lax.axis_size(axis)
    return lax.ppermute(x, axis, [(i, fn(i, n)) for i in range(n)])


def along_tensor(x, k):
    return shifted(x, "tensor", lambda i, n: (i + k) % n)


def along_y(x, k):
    m = BATCH_INNER
    return shifted(x, "batch", lambda i, n: (i // m) * m + (i % m + k) % m)


def along_z(x, k):
    m = BATCH_INNER
    return shifted(x, "batch", lambda i, n: ((i // m + k) % (n // m)) * m + i % m)


def spread(blocks, pos, send):
    m = blocks.shape[0]
    out = [lax.dynamic_index_in_dim(blocks, pos, 0, keepdims=False)]
    for k in range(1, m):
        piece = lax.dynamic_index_in_dim(blocks, (pos + k) % m, 0, keepdims=False)
        out.append(send(piece, k))
    return out


def gather_from(x, pos, m, send):
    out = [x] + [send(x, k) for k in range(1, m)]
    order = (pos - jnp.arange(m)) % m
    return jnp.take(jnp.stack(out), order, axis=0)


def passed_along(block, axis, distance):
    devices = range(lax.axis_size(axis))
    route = [(i - distance, i) for i in devices if i - distance in devices]
    return lax.ppermute(block, axis, route)


def shards(
    hidden, norm_gain, w_query, key_value_weight, w_out, key_value_cache, owner_slot, accepted
):
    f32, bf16 = jnp.float32, jnp.bfloat16
    rounds, rows_local, width_local = hidden.shape
    n_segment = lax.axis_size("segment")
    segment = lax.axis_index("segment")
    tensor = lax.axis_index("tensor")
    group = lax.axis_index("batch")
    requests = owner_slot.shape[0]
    rows_total = requests * DRAFT_BLOCK
    slots_local = key_value_cache.shape[1]
    kv_local = key_value_cache.shape[2]
    query_cols = w_query.shape[2]
    kv_cols = key_value_weight.shape[2]
    block = rounds * DRAFT_BLOCK
    own_rows = slots_local * block
    req_local = rows_local // DRAFT_BLOCK
    scale = HEAD_SIZE ** (-0.5)
    gain = norm_gain[0].astype(f32)
    cache_local = key_value_cache[0]

    onehot = (owner_slot[None, :] == jnp.arange(requests)[:, None]).astype(jnp.int32)
    inverse = jnp.sum(onehot * jnp.arange(requests)[None, :], axis=1)
    acc_slot = jnp.sum(onehot[None] * accepted[:, None, :], axis=2)
    acc_own = lax.dynamic_slice_in_dim(acc_slot, group * slots_local, slots_local, 1)

    rr = jnp.arange(rounds)
    jj = jnp.arange(DRAFT_BLOCK)
    sort_index = (
        rr[None, :, None] * rows_total + inverse[:, None, None] * DRAFT_BLOCK + jj[None, None, :]
    ).reshape(-1)
    own_req = tensor * req_local + jnp.arange(req_local)
    own_index = (
        owner_slot[own_req][None, :, None] * block + rr[:, None, None] * DRAFT_BLOCK + jj[None, None, :]
    ).reshape(-1)

    pos = jnp.arange(block)
    r2 = pos // DRAFT_BLOCK
    place = pos % DRAFT_BLOCK
    acc_pos = acc_own[r2, :].T
    earlier = (r2[None, None, None, :] < rr[None, :, None, None]) & (
        place[None, None, None, :] < acc_pos[:, None, None, :]
    )
    same = (r2[None, :] == rr[:, None])[:, None, :] & (place[None, None, :] <= jj[None, :, None])
    valid = earlier | same[None]
    keep = place[None, :] < acc_pos

    n_tensor = lax.axis_size("tensor")
    n_y = BATCH_INNER
    n_z = lax.axis_size("batch") // n_y
    z_pos = group // n_y
    y_pos = group % n_y

    back_index = (
        owner_slot[None, :, None] * block + rr[:, None, None] * DRAFT_BLOCK + jj[None, None, :]
    ).reshape(-1)

    def layer(x_sorted, last):
        xf = x_sorted.astype(f32)
        sq = jnp.sum(xf * xf, axis=1, keepdims=True)
        sq_hi = sq.astype(bf16)
        sq_lo = (sq - sq_hi.astype(f32)).astype(bf16)
        xg = (xf * gain[None, :]).astype(bf16)
        cut = (query_cols // 2 + kv_cols // 2) // 128 * 128
        first_half = jnp.dot(xg, w_query[0, :, :cut], preferred_element_type=f32).astype(bf16)
        rest = jnp.dot(xg, w_query[0, :, cut:], preferred_element_type=f32)
        second = jnp.dot(xg, key_value_weight[0], preferred_element_type=f32)
        rest = jnp.concatenate([rest.astype(bf16), second.astype(bf16), sq_hi, sq_lo], axis=1)
        first_y = first_half.reshape(n_z, n_y, own_rows, cut).transpose(1, 0, 2, 3)
        first_z = rest.reshape(n_z, n_y, own_rows, rest.shape[1])
        part_a = sum(r.astype(f32) for r in spread(first_y, y_pos, along_y)).astype(bf16)
        part_b = sum(r.astype(f32) for r in spread(first_z, z_pos, along_z))
        total_a = sum(r.astype(f32) for r in spread(part_a, z_pos, along_z))
        total_b = sum(spread(part_b, y_pos, along_y))
        total = jnp.concatenate([total_a, total_b], axis=1)
        total_sq = total[:, query_cols + kv_cols] + total[:, query_cols + kv_cols + 1]
        inv = lax.rsqrt(total_sq / MODEL_WIDTH + 1e-05)[:, None]
        query = (total[:, :query_cols] * inv).astype(bf16)
        keyval = (total[:, query_cols : query_cols + kv_cols] * inv).astype(bf16)
        query_heads = query.reshape(
            slots_local, rounds, DRAFT_BLOCK, kv_local, GROUP_HEADS, HEAD_SIZE
        )
        fresh = keyval.reshape(slots_local, block, kv_local, 2 * HEAD_SIZE).transpose(0, 2, 1, 3)
        s_cache = jnp.einsum(
            "srjhgd,shld->shgrjl", query_heads, cache_local[..., :HEAD_SIZE],
            preferred_element_type=f32,
        ) * scale
        s_fresh = jnp.einsum(
            "srjhgd,shld->shgrjl", query_heads, fresh[..., :HEAD_SIZE],
            preferred_element_type=f32,
        ) * scale
        s_fresh = jnp.where(valid[:, None, None], s_fresh, -1e30)
        scores = jnp.concatenate([s_cache, s_fresh], axis=-1)
        weights = jax.nn.softmax(scores, axis=-1).astype(bf16)
        values = jnp.concatenate([cache_local[..., HEAD_SIZE:], fresh[..., HEAD_SIZE:]], axis=2)
        attended = jnp.einsum(
            "shgrjl,shld->srjhgd", weights, values, preferred_element_type=f32
        )
        attended = attended.astype(bf16).reshape(own_rows, query_cols)
        by_z = gather_from(attended, z_pos, n_z, along_z)
        by_zy = gather_from(by_z, y_pos, n_y, along_y)
        gathered = by_zy.transpose(1, 0, 2, 3).reshape(-1, query_cols)
        partial = jnp.dot(gathered, w_out[0], preferred_element_type=f32)
        ext_new = jnp.where(keep[:, None, :, None], fresh, jnp.zeros_like(fresh))
        if last:
            natural = jnp.take(partial.astype(bf16), back_index, axis=0)
            pieces = natural.reshape(rounds, n_tensor, rows_local, width_local).transpose(1, 0, 2, 3)
            mine = sum(r.astype(f32) for r in spread(pieces, tensor, along_tensor))
            x_own = jnp.take(xf, own_index, axis=0).reshape(rounds, rows_local, width_local)
            return None, (x_own + mine).astype(bf16), ext_new
        quarter = partial.shape[0] // n_tensor
        pieces = partial.astype(bf16).reshape(n_tensor, quarter, width_local)
        mine = sum(r.astype(f32) for r in spread(pieces, tensor, along_tensor))
        x_mine = lax.dynamic_index_in_dim(
            xf.reshape(n_tensor, quarter, width_local), tensor, 0, keepdims=False
        )
        x_mine = (x_mine + mine).astype(bf16)
        x_new = gather_from(x_mine, tensor, n_tensor, along_tensor).reshape(-1, width_local)
        rec_new = jnp.take(x_new, own_index, axis=0).reshape(rounds, rows_local, width_local)
        return x_new, rec_new, ext_new

    rows_all = gather_from(hidden, tensor, n_tensor, along_tensor)
    rows_all = rows_all.transpose(1, 0, 2, 3).reshape(-1, width_local)
    x = jnp.take(rows_all, sort_index, axis=0)
    record = None
    ext = None
    for step in range(n_segment):
        x_new, rec_new, ext_new = layer(x, step + 1 == n_segment)
        if step == 0:
            record, ext = rec_new, ext_new
        else:
            active = segment == step
            record = jnp.where(active, rec_new, record)
            ext = jnp.where(active, ext_new, ext)
        if step + 1 < n_segment:
            x = passed_along(x_new, "segment", 1)
    return (record[None], ext[None])


def solution(mesh):
    in_specs = (
        P(None, "tensor", "batch"),
        P("segment", "batch"),
        P("segment", "batch", "tensor"),
        P("segment", "batch", "tensor"),
        P("segment", "tensor", "batch"),
        P("segment", "batch", "tensor", None, None),
        P(),
        P(),
    )
    out_specs = (P("segment", None, "tensor", "batch"), P("segment", "batch", "tensor", None, None))
    return jax.shard_map(shards, mesh=mesh, in_specs=in_specs, out_specs=out_specs, check_vma=False)
```

```python
import jax
import jax.numpy as jnp
from jax import lax
from jax.sharding import PartitionSpec as P

MODEL_WIDTH = 16384
HEAD_SIZE = 128
DRAFT_BLOCK = 4
DECODE_ROUNDS = 3
GROUP_HEADS = 8


BATCH_INNER = 4


def shifted(x, axis, fn):
    n = lax.axis_size(axis)
    return lax.ppermute(x, axis, [(i, fn(i, n)) for i in range(n)])


def along_tensor(x, k):
    return shifted(x, "tensor", lambda i, n: (i + k) % n)


def along_y(x, k):
    m = BATCH_INNER
    return shifted(x, "batch", lambda i, n: (i // m) * m + (i % m + k) % m)


def along_z(x, k):
    m = BATCH_INNER
    return shifted(x, "batch", lambda i, n: ((i // m + k) % (n // m)) * m + i % m)


def spread(blocks, pos, send):
    m = blocks.shape[0]
    out = [lax.dynamic_index_in_dim(blocks, pos, 0, keepdims=False)]
    for k in range(1, m):
        piece = lax.dynamic_index_in_dim(blocks, (pos + k) % m, 0, keepdims=False)
        out.append(send(piece, k))
    return out


def gather_from(x, pos, m, send):
    out = [x] + [send(x, k) for k in range(1, m)]
    order = (pos - jnp.arange(m)) % m
    return jnp.take(jnp.stack(out), order, axis=0)


def passed_along(block, axis, distance):
    devices = range(lax.axis_size(axis))
    route = [(i - distance, i) for i in devices if i - distance in devices]
    return lax.ppermute(block, axis, route)


def shards(
    hidden, norm_gain, w_query, key_value_weight, w_out, key_value_cache, owner_slot, accepted
):
    f32, bf16 = jnp.float32, jnp.bfloat16
    rounds, rows_local, width_local = hidden.shape
    n_segment = lax.axis_size("segment")
    segment = lax.axis_index("segment")
    tensor = lax.axis_index("tensor")
    group = lax.axis_index("batch")
    requests = owner_slot.shape[0]
    rows_total = requests * DRAFT_BLOCK
    slots_local = key_value_cache.shape[1]
    kv_local = key_value_cache.shape[2]
    query_cols = w_query.shape[2]
    kv_cols = key_value_weight.shape[2]
    block = rounds * DRAFT_BLOCK
    own_rows = slots_local * block
    req_local = rows_local // DRAFT_BLOCK
    scale = HEAD_SIZE ** (-0.5)
    gain = norm_gain[0].astype(f32)
    cache_local = key_value_cache[0]

    onehot = (owner_slot[None, :] == jnp.arange(requests)[:, None]).astype(jnp.int32)
    inverse = jnp.sum(onehot * jnp.arange(requests)[None, :], axis=1)
    acc_slot = jnp.sum(onehot[None] * accepted[:, None, :], axis=2)
    acc_own = lax.dynamic_slice_in_dim(acc_slot, group * slots_local, slots_local, 1)

    rr = jnp.arange(rounds)
    jj = jnp.arange(DRAFT_BLOCK)
    sort_index = (
        rr[None, :, None] * rows_total + inverse[:, None, None] * DRAFT_BLOCK + jj[None, None, :]
    ).reshape(-1)
    own_req = tensor * req_local + jnp.arange(req_local)
    own_index = (
        owner_slot[own_req][None, :, None] * block + rr[:, None, None] * DRAFT_BLOCK + jj[None, None, :]
    ).reshape(-1)

    pos = jnp.arange(block)
    r2 = pos // DRAFT_BLOCK
    place = pos % DRAFT_BLOCK
    acc_pos = acc_own[r2, :].T
    earlier = (r2[None, None, None, :] < rr[None, :, None, None]) & (
        place[None, None, None, :] < acc_pos[:, None, None, :]
    )
    same = (r2[None, :] == rr[:, None])[:, None, :] & (place[None, None, :] <= jj[None, :, None])
    valid = earlier | same[None]
    keep = place[None, :] < acc_pos

    n_tensor = lax.axis_size("tensor")
    n_y = BATCH_INNER
    n_z = lax.axis_size("batch") // n_y
    z_pos = group // n_y
    y_pos = group % n_y

    back_index = (
        owner_slot[None, :, None] * block + rr[:, None, None] * DRAFT_BLOCK + jj[None, None, :]
    ).reshape(-1)

    def arrived_at(s):
        b = s // own_rows
        shift_y = (y_pos - b % n_y) % n_y
        shift_z = (z_pos - b // n_y) % n_z
        return (shift_y * n_z + shift_z) * own_rows + s % own_rows

    def layer(x_sorted, last):
        xf = x_sorted.astype(f32)
        sq = jnp.sum(xf * xf, axis=1, keepdims=True)
        sq_hi = sq.astype(bf16)
        sq_lo = (sq - sq_hi.astype(f32)).astype(bf16)
        xg = (xf * gain[None, :]).astype(bf16)
        cut = (query_cols // 2 + kv_cols // 2) // 128 * 128
        first_half = jnp.dot(xg, w_query[0, :, :cut], preferred_element_type=f32).astype(bf16)
        rest = jnp.dot(xg, w_query[0, :, cut:], preferred_element_type=f32)
        second = jnp.dot(xg, key_value_weight[0], preferred_element_type=f32)
        rest = jnp.concatenate([rest.astype(bf16), second.astype(bf16), sq_hi, sq_lo], axis=1)
        first_y = first_half.reshape(n_z, n_y, own_rows, cut).transpose(1, 0, 2, 3)
        first_z = rest.reshape(n_z, n_y, own_rows, rest.shape[1])
        part_a = sum(r.astype(f32) for r in spread(first_y, y_pos, along_y)).astype(bf16)
        part_b = sum(r.astype(f32) for r in spread(first_z, z_pos, along_z))
        total_a = sum(r.astype(f32) for r in spread(part_a, z_pos, along_z))
        total_b = sum(spread(part_b, y_pos, along_y))
        total = jnp.concatenate([total_a, total_b], axis=1)
        total_sq = total[:, query_cols + kv_cols] + total[:, query_cols + kv_cols + 1]
        inv = lax.rsqrt(total_sq / MODEL_WIDTH + 1e-05)[:, None]
        query = (total[:, :query_cols] * inv).astype(bf16)
        keyval = (total[:, query_cols : query_cols + kv_cols] * inv).astype(bf16)
        query_heads = query.reshape(
            slots_local, rounds, DRAFT_BLOCK, kv_local, GROUP_HEADS, HEAD_SIZE
        )
        fresh = keyval.reshape(slots_local, block, kv_local, 2 * HEAD_SIZE).transpose(0, 2, 1, 3)
        s_cache = jnp.einsum(
            "srjhgd,shld->shgrjl", query_heads, cache_local[..., :HEAD_SIZE],
            preferred_element_type=f32,
        ) * scale
        s_fresh = jnp.einsum(
            "srjhgd,shld->shgrjl", query_heads, fresh[..., :HEAD_SIZE],
            preferred_element_type=f32,
        ) * scale
        s_fresh = jnp.where(valid[:, None, None], s_fresh, -1e30)
        scores = jnp.concatenate([s_cache, s_fresh], axis=-1)
        weights = jax.nn.softmax(scores, axis=-1).astype(bf16)
        values = jnp.concatenate([cache_local[..., HEAD_SIZE:], fresh[..., HEAD_SIZE:]], axis=2)
        attended = jnp.einsum(
            "shgrjl,shld->srjhgd", weights, values, preferred_element_type=f32
        )
        attended = attended.astype(bf16).reshape(own_rows, query_cols)
        by_z = jnp.stack([attended] + [along_z(attended, k) for k in range(1, n_z)])
        by_zy = jnp.stack([by_z] + [along_y(by_z, k) for k in range(1, n_y)])
        gathered = by_zy.reshape(-1, query_cols)
        partial = jnp.dot(gathered, w_out[0], preferred_element_type=f32).astype(bf16)
        ext_new = jnp.where(keep[:, None, :, None], fresh, jnp.zeros_like(fresh))
        if last:
            natural = jnp.take(partial, arrived_at(back_index), axis=0)
            pieces = natural.reshape(rounds, n_tensor, rows_local, width_local).transpose(1, 0, 2, 3)
            mine = sum(r.astype(f32) for r in spread(pieces, tensor, along_tensor))
            x_own = jnp.take(xf, own_index, axis=0).reshape(rounds, rows_local, width_local)
            return None, (x_own + mine).astype(bf16), ext_new
        quarter = partial.shape[0] // n_tensor
        in_order = jnp.take(partial, arrived_at(jnp.arange(partial.shape[0])), axis=0)
        pieces = in_order.reshape(n_tensor, quarter, width_local)
        mine = sum(r.astype(f32) for r in spread(pieces, tensor, along_tensor))
        x_mine = lax.dynamic_index_in_dim(
            xf.reshape(n_tensor, quarter, width_local), tensor, 0, keepdims=False
        )
        x_mine = (x_mine + mine).astype(bf16)
        x_new = gather_from(x_mine, tensor, n_tensor, along_tensor).reshape(-1, width_local)
        rec_new = jnp.take(x_new, own_index, axis=0).reshape(rounds, rows_local, width_local)
        return x_new, rec_new, ext_new

    rows_all = gather_from(hidden, tensor, n_tensor, along_tensor)
    rows_all = rows_all.transpose(1, 0, 2, 3).reshape(-1, width_local)
    x = jnp.take(rows_all, sort_index, axis=0)
    record = None
    ext = None
    for step in range(n_segment):
        x_new, rec_new, ext_new = layer(x, step + 1 == n_segment)
        if step == 0:
            record, ext = rec_new, ext_new
        else:
            active = segment == step
            record = jnp.where(active, rec_new, record)
            ext = jnp.where(active, ext_new, ext)
        if step + 1 < n_segment:
            x = passed_along(x_new, "segment", 1)
    return (record[None], ext[None])


def solution(mesh):
    in_specs = (
        P(None, "tensor", "batch"),
        P("segment", "batch"),
        P("segment", "batch", "tensor"),
        P("segment", "batch", "tensor"),
        P("segment", "tensor", "batch"),
        P("segment", "batch", "tensor", None, None),
        P(),
        P(),
    )
    out_specs = (P("segment", None, "tensor", "batch"), P("segment", "batch", "tensor", None, None))
    return jax.shard_map(shards, mesh=mesh, in_specs=in_specs, out_specs=out_specs, check_vma=False)
```

```python
import jax
import jax.numpy as jnp
from jax import lax
from jax.sharding import PartitionSpec as P

MODEL_WIDTH = 16384
HEAD_SIZE = 128
DRAFT_BLOCK = 4
DECODE_ROUNDS = 3
GROUP_HEADS = 8


BATCH_INNER = 4


def shifted(x, axis, fn):
    n = lax.axis_size(axis)
    return lax.ppermute(x, axis, [(i, fn(i, n)) for i in range(n)])


def along_tensor(x, k):
    return shifted(x, "tensor", lambda i, n: (i + k) % n)


def along_y(x, k):
    m = BATCH_INNER
    return shifted(x, "batch", lambda i, n: (i // m) * m + (i % m + k) % m)


def along_z(x, k):
    m = BATCH_INNER
    return shifted(x, "batch", lambda i, n: ((i // m + k) % (n // m)) * m + i % m)


def spread(blocks, pos, send):
    m = blocks.shape[0]
    out = [lax.dynamic_index_in_dim(blocks, pos, 0, keepdims=False)]
    for k in range(1, m):
        piece = lax.dynamic_index_in_dim(blocks, (pos + k) % m, 0, keepdims=False)
        out.append(send(piece, k))
    return out


def gather_from(x, pos, m, send):
    out = [x] + [send(x, k) for k in range(1, m)]
    order = (pos - jnp.arange(m)) % m
    return jnp.take(jnp.stack(out), order, axis=0)


def passed_along(block, axis, distance):
    devices = range(lax.axis_size(axis))
    route = [(i - distance, i) for i in devices if i - distance in devices]
    return lax.ppermute(block, axis, route)


def shards(
    hidden, norm_gain, w_query, key_value_weight, w_out, key_value_cache, owner_slot, accepted
):
    f32, bf16 = jnp.float32, jnp.bfloat16
    rounds, rows_local, width_local = hidden.shape
    n_segment = lax.axis_size("segment")
    segment = lax.axis_index("segment")
    tensor = lax.axis_index("tensor")
    group = lax.axis_index("batch")
    requests = owner_slot.shape[0]
    rows_total = requests * DRAFT_BLOCK
    slots_local = key_value_cache.shape[1]
    kv_local = key_value_cache.shape[2]
    query_cols = w_query.shape[2]
    kv_cols = key_value_weight.shape[2]
    block = rounds * DRAFT_BLOCK
    own_rows = slots_local * block
    req_local = rows_local // DRAFT_BLOCK
    scale = HEAD_SIZE ** (-0.5)
    gain = norm_gain[0].astype(f32)
    cache_local = key_value_cache[0]

    onehot = (owner_slot[None, :] == jnp.arange(requests)[:, None]).astype(jnp.int32)
    inverse = jnp.sum(onehot * jnp.arange(requests)[None, :], axis=1)
    acc_slot = jnp.sum(onehot[None] * accepted[:, None, :], axis=2)
    acc_own = lax.dynamic_slice_in_dim(acc_slot, group * slots_local, slots_local, 1)

    rr = jnp.arange(rounds)
    jj = jnp.arange(DRAFT_BLOCK)
    sort_index = (
        rr[None, :, None] * rows_total + inverse[:, None, None] * DRAFT_BLOCK + jj[None, None, :]
    ).reshape(-1)
    own_req = tensor * req_local + jnp.arange(req_local)
    own_index = (
        owner_slot[own_req][None, :, None] * block + rr[:, None, None] * DRAFT_BLOCK + jj[None, None, :]
    ).reshape(-1)

    pos = jnp.arange(block)
    r2 = pos // DRAFT_BLOCK
    place = pos % DRAFT_BLOCK
    acc_pos = acc_own[r2, :].T
    earlier = (r2[None, None, None, :] < rr[None, :, None, None]) & (
        place[None, None, None, :] < acc_pos[:, None, None, :]
    )
    same = (r2[None, :] == rr[:, None])[:, None, :] & (place[None, None, :] <= jj[None, :, None])
    valid = earlier | same[None]
    keep = place[None, :] < acc_pos

    n_tensor = lax.axis_size("tensor")
    n_y = BATCH_INNER
    n_z = lax.axis_size("batch") // n_y
    z_pos = group // n_y
    y_pos = group % n_y

    back_index = (
        owner_slot[None, :, None] * block + rr[:, None, None] * DRAFT_BLOCK + jj[None, None, :]
    ).reshape(-1)

    def arrived_at(s):
        b = s // own_rows
        shift_y = (y_pos - b % n_y) % n_y
        shift_z = (z_pos - b // n_y) % n_z
        return (shift_y * n_z + shift_z) * own_rows + s % own_rows

    def layer(x_sorted, last):
        xf = x_sorted.astype(f32)
        sq = jnp.sum(xf * xf, axis=1, keepdims=True)
        sq_hi = sq.astype(bf16)
        sq_lo = (sq - sq_hi.astype(f32)).astype(bf16)
        xg = (xf * gain[None, :]).astype(bf16)
        cut = (query_cols // 2 + kv_cols // 2) // 128 * 128
        first_half = jnp.dot(xg, w_query[0, :, :cut], preferred_element_type=f32).astype(bf16)
        rest = jnp.dot(xg, w_query[0, :, cut:], preferred_element_type=f32)
        second = jnp.dot(xg, key_value_weight[0], preferred_element_type=f32)
        rest = jnp.concatenate([rest.astype(bf16), second.astype(bf16), sq_hi, sq_lo], axis=1)
        first_y = first_half.reshape(n_z, n_y, own_rows, cut).transpose(1, 0, 2, 3)
        first_z = rest.reshape(n_z, n_y, own_rows, rest.shape[1])
        part_a = sum(r.astype(f32) for r in spread(first_y, y_pos, along_y)).astype(bf16)
        part_b = sum(r.astype(f32) for r in spread(first_z, z_pos, along_z))
        total_a = sum(r.astype(f32) for r in spread(part_a, z_pos, along_z))
        total_b = sum(spread(part_b, y_pos, along_y))
        total = jnp.concatenate([total_a, total_b], axis=1)
        total_sq = total[:, query_cols + kv_cols] + total[:, query_cols + kv_cols + 1]
        inv = lax.rsqrt(total_sq / MODEL_WIDTH + 1e-05)[:, None]
        query = (total[:, :query_cols] * inv).astype(bf16)
        keyval = (total[:, query_cols : query_cols + kv_cols] * inv).astype(bf16)
        query_heads = query.reshape(
            slots_local, rounds, DRAFT_BLOCK, kv_local, GROUP_HEADS, HEAD_SIZE
        )
        fresh = keyval.reshape(slots_local, block, kv_local, 2 * HEAD_SIZE).transpose(0, 2, 1, 3)
        s_cache = jnp.einsum(
            "srjhgd,shld->shgrjl", query_heads, cache_local[..., :HEAD_SIZE],
            preferred_element_type=f32,
        ) * scale
        s_fresh = jnp.einsum(
            "srjhgd,shld->shgrjl", query_heads, fresh[..., :HEAD_SIZE],
            preferred_element_type=f32,
        ) * scale
        s_fresh = jnp.where(valid[:, None, None], s_fresh, -1e30)
        scores = jnp.concatenate([s_cache, s_fresh], axis=-1)
        weights = jax.nn.softmax(scores, axis=-1).astype(bf16)
        values = jnp.concatenate([cache_local[..., HEAD_SIZE:], fresh[..., HEAD_SIZE:]], axis=2)
        attended = jnp.einsum(
            "shgrjl,shld->srjhgd", weights, values, preferred_element_type=f32
        )
        attended = attended.astype(bf16).reshape(own_rows, query_cols)
        by_z = jnp.stack([attended] + [along_z(attended, k) for k in range(1, n_z)])
        by_zy = jnp.stack([by_z] + [along_y(by_z, k) for k in range(1, n_y)])
        gathered = by_zy.reshape(-1, query_cols)
        partial = jnp.dot(gathered, w_out[0], preferred_element_type=f32).astype(bf16)
        ext_new = jnp.where(keep[:, None, :, None], fresh, jnp.zeros_like(fresh))
        if last:
            natural = jnp.take(partial, arrived_at(back_index), axis=0)
            pieces = natural.reshape(rounds, n_tensor, rows_local, width_local).transpose(1, 0, 2, 3)
            mine = sum(r.astype(f32) for r in spread(pieces, tensor, along_tensor))
            x_own = jnp.take(xf, own_index, axis=0).reshape(rounds, rows_local, width_local)
            return None, (x_own + mine).astype(bf16), ext_new
        quarter = partial.shape[0] // n_tensor
        in_order = jnp.take(partial, arrived_at(jnp.arange(partial.shape[0])), axis=0)
        pieces = in_order.reshape(n_tensor, quarter, width_local)
        mine = sum(r.astype(f32) for r in spread(pieces, tensor, along_tensor))
        x_mine = lax.dynamic_index_in_dim(
            xf.reshape(n_tensor, quarter, width_local), tensor, 0, keepdims=False
        )
        x_mine = (x_mine + mine).astype(bf16)
        x_new = gather_from(x_mine, tensor, n_tensor, along_tensor).reshape(-1, width_local)
        rec_new = jnp.take(x_new, own_index, axis=0).reshape(rounds, rows_local, width_local)
        return x_new, rec_new, ext_new

    arrived = jnp.stack([hidden] + [along_tensor(hidden, k) for k in range(1, n_tensor)])
    arrived = arrived.reshape(-1, width_local)
    src_t = inverse // req_local
    shift_t = (tensor - src_t) % n_tensor
    within = (inverse % req_local) * DRAFT_BLOCK
    arrival_index = (
        ((shift_t[:, None, None] * rounds + rr[None, :, None]) * rows_local)
        + within[:, None, None]
        + jj[None, None, :]
    ).reshape(-1)
    x = jnp.take(arrived, arrival_index, axis=0)
    record = None
    ext = None
    for step in range(n_segment):
        x_new, rec_new, ext_new = layer(x, step + 1 == n_segment)
        if step == 0:
            record, ext = rec_new, ext_new
        else:
            active = segment == step
            record = jnp.where(active, rec_new, record)
            ext = jnp.where(active, ext_new, ext)
        if step + 1 < n_segment:
            x = passed_along(x_new, "segment", 1)
    return (record[None], ext[None])


def solution(mesh):
    in_specs = (
        P(None, "tensor", "batch"),
        P("segment", "batch"),
        P("segment", "batch", "tensor"),
        P("segment", "batch", "tensor"),
        P("segment", "tensor", "batch"),
        P("segment", "batch", "tensor", None, None),
        P(),
        P(),
    )
    out_specs = (P("segment", None, "tensor", "batch"), P("segment", "batch", "tensor", None, None))
    return jax.shard_map(shards, mesh=mesh, in_specs=in_specs, out_specs=out_specs, check_vma=False)
```

```python
import jax
import jax.numpy as jnp
from jax import lax
from jax.sharding import PartitionSpec as P

MODEL_WIDTH = 16384
HEAD_SIZE = 128
DRAFT_BLOCK = 4
DECODE_ROUNDS = 3
GROUP_HEADS = 8


BATCH_INNER = 4


def shifted(x, axis, fn):
    n = lax.axis_size(axis)
    return lax.ppermute(x, axis, [(i, fn(i, n)) for i in range(n)])


def along_tensor(x, k):
    return shifted(x, "tensor", lambda i, n: (i + k) % n)


def along_y(x, k):
    m = BATCH_INNER
    return shifted(x, "batch", lambda i, n: (i // m) * m + (i % m + k) % m)


def along_z(x, k):
    m = BATCH_INNER
    return shifted(x, "batch", lambda i, n: ((i // m + k) % (n // m)) * m + i % m)


def spread(blocks, pos, send, axis=0):
    m = blocks.shape[axis]
    out = [lax.dynamic_index_in_dim(blocks, pos, axis, keepdims=False)]
    for k in range(1, m):
        piece = lax.dynamic_index_in_dim(blocks, (pos + k) % m, axis, keepdims=False)
        out.append(send(piece, k))
    return out


def gather_from(x, pos, m, send):
    out = [x] + [send(x, k) for k in range(1, m)]
    order = (pos - jnp.arange(m)) % m
    return jnp.take(jnp.stack(out), order, axis=0)


def passed_along(block, axis, distance):
    devices = range(lax.axis_size(axis))
    route = [(i - distance, i) for i in devices if i - distance in devices]
    return lax.ppermute(block, axis, route)


def shards(
    hidden, norm_gain, w_query, key_value_weight, w_out, key_value_cache, owner_slot, accepted
):
    f32, bf16 = jnp.float32, jnp.bfloat16
    rounds, rows_local, width_local = hidden.shape
    n_segment = lax.axis_size("segment")
    segment = lax.axis_index("segment")
    tensor = lax.axis_index("tensor")
    group = lax.axis_index("batch")
    requests = owner_slot.shape[0]
    rows_total = requests * DRAFT_BLOCK
    slots_local = key_value_cache.shape[1]
    kv_local = key_value_cache.shape[2]
    query_cols = w_query.shape[2]
    kv_cols = key_value_weight.shape[2]
    block = rounds * DRAFT_BLOCK
    own_rows = slots_local * block
    req_local = rows_local // DRAFT_BLOCK
    scale = HEAD_SIZE ** (-0.5)
    gain = norm_gain[0].astype(f32)
    cache_local = key_value_cache[0]

    onehot = (owner_slot[None, :] == jnp.arange(requests)[:, None]).astype(jnp.int32)
    inverse = jnp.sum(onehot * jnp.arange(requests)[None, :], axis=1)
    acc_slot = jnp.sum(onehot[None] * accepted[:, None, :], axis=2)
    acc_own = lax.dynamic_slice_in_dim(acc_slot, group * slots_local, slots_local, 1)

    rr = jnp.arange(rounds)
    jj = jnp.arange(DRAFT_BLOCK)
    sort_index = (
        rr[None, :, None] * rows_total + inverse[:, None, None] * DRAFT_BLOCK + jj[None, None, :]
    ).reshape(-1)
    own_req = tensor * req_local + jnp.arange(req_local)
    own_index = (
        owner_slot[own_req][None, :, None] * block + rr[:, None, None] * DRAFT_BLOCK + jj[None, None, :]
    ).reshape(-1)

    pos = jnp.arange(block)
    r2 = pos // DRAFT_BLOCK
    place = pos % DRAFT_BLOCK
    acc_pos = acc_own[r2, :].T
    earlier = (r2[None, None, None, :] < rr[None, :, None, None]) & (
        place[None, None, None, :] < acc_pos[:, None, None, :]
    )
    same = (r2[None, :] == rr[:, None])[:, None, :] & (place[None, None, :] <= jj[None, :, None])
    valid = earlier | same[None]
    keep = place[None, :] < acc_pos

    n_tensor = lax.axis_size("tensor")
    n_y = BATCH_INNER
    n_z = lax.axis_size("batch") // n_y
    z_pos = group // n_y
    y_pos = group % n_y

    back_index = (
        owner_slot[None, :, None] * block + rr[:, None, None] * DRAFT_BLOCK + jj[None, None, :]
    ).reshape(-1)

    def arrived_at(s):
        b = s // own_rows
        shift_y = (y_pos - b % n_y) % n_y
        shift_z = (z_pos - b // n_y) % n_z
        return (shift_y * n_z + shift_z) * own_rows + s % own_rows

    def layer(x_sorted, last):
        xf = x_sorted.astype(f32)
        sq = jnp.sum(xf * xf, axis=1, keepdims=True)
        sq_hi = sq.astype(bf16)
        sq_lo = (sq - sq_hi.astype(f32)).astype(bf16)
        xg = (xf * gain[None, :]).astype(bf16)
        cut = (query_cols // 2 + kv_cols // 2) // 128 * 128
        first_half = jnp.dot(xg, w_query[0, :, :cut], preferred_element_type=f32).astype(bf16)
        rest = jnp.dot(xg, w_query[0, :, cut:], preferred_element_type=f32)
        second = jnp.dot(xg, key_value_weight[0], preferred_element_type=f32)
        rest = jnp.concatenate([rest.astype(bf16), second.astype(bf16), sq_hi, sq_lo], axis=1)
        first_y = first_half.reshape(n_z, n_y, own_rows, cut)
        first_z = rest.reshape(n_z, n_y, own_rows, rest.shape[1])
        part_a = sum(r.astype(f32) for r in spread(first_y, y_pos, along_y, 1)).astype(bf16)
        part_b = sum(r.astype(f32) for r in spread(first_z, z_pos, along_z))
        total_a = sum(r.astype(f32) for r in spread(part_a, z_pos, along_z))
        total_b = sum(spread(part_b, y_pos, along_y))
        total = jnp.concatenate([total_a, total_b], axis=1)
        total_sq = total[:, query_cols + kv_cols] + total[:, query_cols + kv_cols + 1]
        inv = lax.rsqrt(total_sq / MODEL_WIDTH + 1e-05)[:, None]
        query = (total[:, :query_cols] * inv).astype(bf16)
        keyval = (total[:, query_cols : query_cols + kv_cols] * inv).astype(bf16)
        query_heads = query.reshape(
            slots_local, rounds, DRAFT_BLOCK, kv_local, GROUP_HEADS, HEAD_SIZE
        )
        fresh = keyval.reshape(slots_local, block, kv_local, 2 * HEAD_SIZE).transpose(0, 2, 1, 3)
        s_cache = jnp.einsum(
            "srjhgd,shld->shgrjl", query_heads, cache_local[..., :HEAD_SIZE],
            preferred_element_type=f32,
        ) * scale
        s_fresh = jnp.einsum(
            "srjhgd,shld->shgrjl", query_heads, fresh[..., :HEAD_SIZE],
            preferred_element_type=f32,
        ) * scale
        s_fresh = jnp.where(valid[:, None, None], s_fresh, -1e30)
        scores = jnp.concatenate([s_cache, s_fresh], axis=-1)
        weights = jax.nn.softmax(scores, axis=-1).astype(bf16)
        values = jnp.concatenate([cache_local[..., HEAD_SIZE:], fresh[..., HEAD_SIZE:]], axis=2)
        attended = jnp.einsum(
            "shgrjl,shld->srjhgd", weights, values, preferred_element_type=f32
        )
        attended = attended.astype(bf16).reshape(own_rows, query_cols)
        by_z = jnp.stack([attended] + [along_z(attended, k) for k in range(1, n_z)])
        by_zy = jnp.stack([by_z] + [along_y(by_z, k) for k in range(1, n_y)])
        gathered = by_zy.reshape(-1, query_cols)
        partial = jnp.dot(gathered, w_out[0], preferred_element_type=f32).astype(bf16)
        ext_new = jnp.where(keep[:, None, :, None], fresh, jnp.zeros_like(fresh))
        if last:
            natural = jnp.take(partial, arrived_at(back_index), axis=0)
            pieces = natural.reshape(rounds, n_tensor, rows_local, width_local).transpose(1, 0, 2, 3)
            mine = sum(r.astype(f32) for r in spread(pieces, tensor, along_tensor))
            x_own = jnp.take(xf, own_index, axis=0).reshape(rounds, rows_local, width_local)
            return None, (x_own + mine).astype(bf16), ext_new
        quarter = partial.shape[0] // n_tensor
        in_order = jnp.take(partial, arrived_at(jnp.arange(partial.shape[0])), axis=0)
        pieces = in_order.reshape(n_tensor, quarter, width_local)
        mine = sum(r.astype(f32) for r in spread(pieces, tensor, along_tensor))
        x_mine = lax.dynamic_index_in_dim(
            xf.reshape(n_tensor, quarter, width_local), tensor, 0, keepdims=False
        )
        x_mine = (x_mine + mine).astype(bf16)
        x_new = gather_from(x_mine, tensor, n_tensor, along_tensor).reshape(-1, width_local)
        rec_new = jnp.take(x_new, own_index, axis=0).reshape(rounds, rows_local, width_local)
        return x_new, rec_new, ext_new

    arrived = jnp.stack([hidden] + [along_tensor(hidden, k) for k in range(1, n_tensor)])
    arrived = arrived.reshape(-1, width_local)
    src_t = inverse // req_local
    shift_t = (tensor - src_t) % n_tensor
    within = (inverse % req_local) * DRAFT_BLOCK
    arrival_index = (
        ((shift_t[:, None, None] * rounds + rr[None, :, None]) * rows_local)
        + within[:, None, None]
        + jj[None, None, :]
    ).reshape(-1)
    x = jnp.take(arrived, arrival_index, axis=0)
    record = None
    ext = None
    for step in range(n_segment):
        x_new, rec_new, ext_new = layer(x, step + 1 == n_segment)
        if step == 0:
            record, ext = rec_new, ext_new
        else:
            active = segment == step
            record = jnp.where(active, rec_new, record)
            ext = jnp.where(active, ext_new, ext)
        if step + 1 < n_segment:
            x = passed_along(x_new, "segment", 1)
    return (record[None], ext[None])


def solution(mesh):
    in_specs = (
        P(None, "tensor", "batch"),
        P("segment", "batch"),
        P("segment", "batch", "tensor"),
        P("segment", "batch", "tensor"),
        P("segment", "tensor", "batch"),
        P("segment", "batch", "tensor", None, None),
        P(),
        P(),
    )
    out_specs = (P("segment", None, "tensor", "batch"), P("segment", "batch", "tensor", None, None))
    return jax.shard_map(shards, mesh=mesh, in_specs=in_specs, out_specs=out_specs, check_vma=False)
```

```python
import jax
import jax.numpy as jnp
from jax import lax
from jax.sharding import PartitionSpec as P

MODEL_WIDTH = 16384
HEAD_SIZE = 128
DRAFT_BLOCK = 4
DECODE_ROUNDS = 3
GROUP_HEADS = 8


BATCH_INNER = 4


def shifted(x, axis, fn):
    n = lax.axis_size(axis)
    return lax.ppermute(x, axis, [(i, fn(i, n)) for i in range(n)])


def along_tensor(x, k):
    return shifted(x, "tensor", lambda i, n: (i + k) % n)


def along_y(x, k):
    m = BATCH_INNER
    return shifted(x, "batch", lambda i, n: (i // m) * m + (i % m + k) % m)


def along_z(x, k):
    m = BATCH_INNER
    return shifted(x, "batch", lambda i, n: ((i // m + k) % (n // m)) * m + i % m)


def spread(blocks, pos, send):
    m = blocks.shape[0]
    out = [lax.dynamic_index_in_dim(blocks, pos, 0, keepdims=False)]
    for k in range(1, m):
        piece = lax.dynamic_index_in_dim(blocks, (pos + k) % m, 0, keepdims=False)
        out.append(send(piece, k))
    return out


def gather_from(x, pos, m, send):
    out = [x] + [send(x, k) for k in range(1, m)]
    order = (pos - jnp.arange(m)) % m
    return jnp.take(jnp.stack(out), order, axis=0)


def passed_along(block, axis, distance):
    devices = range(lax.axis_size(axis))
    route = [(i - distance, i) for i in devices if i - distance in devices]
    return lax.ppermute(block, axis, route)


def handed_on(x, step):
    n = lax.axis_size("tensor")
    outs = []
    for k in range(n):
        pairs = [(step * n + t, (step + 1) * n + (t + k) % n) for t in range(n)]
        outs.append(lax.ppermute(x, ("segment", "tensor"), pairs))
    return jnp.stack(outs)


def shards(
    hidden, norm_gain, w_query, key_value_weight, w_out, key_value_cache, owner_slot, accepted
):
    f32, bf16 = jnp.float32, jnp.bfloat16
    rounds, rows_local, width_local = hidden.shape
    n_segment = lax.axis_size("segment")
    segment = lax.axis_index("segment")
    tensor = lax.axis_index("tensor")
    group = lax.axis_index("batch")
    requests = owner_slot.shape[0]
    rows_total = requests * DRAFT_BLOCK
    slots_local = key_value_cache.shape[1]
    kv_local = key_value_cache.shape[2]
    query_cols = w_query.shape[2]
    kv_cols = key_value_weight.shape[2]
    block = rounds * DRAFT_BLOCK
    own_rows = slots_local * block
    req_local = rows_local // DRAFT_BLOCK
    scale = HEAD_SIZE ** (-0.5)
    gain = norm_gain[0].astype(f32)
    cache_local = key_value_cache[0]

    onehot = (owner_slot[None, :] == jnp.arange(requests)[:, None]).astype(jnp.int32)
    inverse = jnp.sum(onehot * jnp.arange(requests)[None, :], axis=1)
    acc_slot = jnp.sum(onehot[None] * accepted[:, None, :], axis=2)
    acc_own = lax.dynamic_slice_in_dim(acc_slot, group * slots_local, slots_local, 1)

    rr = jnp.arange(rounds)
    jj = jnp.arange(DRAFT_BLOCK)
    sort_index = (
        rr[None, :, None] * rows_total + inverse[:, None, None] * DRAFT_BLOCK + jj[None, None, :]
    ).reshape(-1)
    own_req = tensor * req_local + jnp.arange(req_local)
    own_index = (
        owner_slot[own_req][None, :, None] * block + rr[:, None, None] * DRAFT_BLOCK + jj[None, None, :]
    ).reshape(-1)

    pos = jnp.arange(block)
    r2 = pos // DRAFT_BLOCK
    place = pos % DRAFT_BLOCK
    acc_pos = acc_own[r2, :].T
    earlier = (r2[None, None, None, :] < rr[None, :, None, None]) & (
        place[None, None, None, :] < acc_pos[:, None, None, :]
    )
    same = (r2[None, :] == rr[:, None])[:, None, :] & (place[None, None, :] <= jj[None, :, None])
    valid = earlier | same[None]
    keep = place[None, :] < acc_pos

    n_tensor = lax.axis_size("tensor")
    n_y = BATCH_INNER
    n_z = lax.axis_size("batch") // n_y
    z_pos = group // n_y
    y_pos = group % n_y

    back_index = (
        owner_slot[None, :, None] * block + rr[:, None, None] * DRAFT_BLOCK + jj[None, None, :]
    ).reshape(-1)

    def arrived_at(s):
        b = s // own_rows
        shift_y = (y_pos - b % n_y) % n_y
        shift_z = (z_pos - b // n_y) % n_z
        return (shift_y * n_z + shift_z) * own_rows + s % own_rows

    def layer(x_sorted):
        xf = x_sorted.astype(f32)
        sq = jnp.sum(xf * xf, axis=1, keepdims=True)
        sq_hi = sq.astype(bf16)
        sq_lo = (sq - sq_hi.astype(f32)).astype(bf16)
        xg = (xf * gain[None, :]).astype(bf16)
        cut = (query_cols // 2 + kv_cols // 2) // 128 * 128
        first_half = jnp.dot(xg, w_query[0, :, :cut], preferred_element_type=f32).astype(bf16)
        rest = jnp.dot(xg, w_query[0, :, cut:], preferred_element_type=f32)
        second = jnp.dot(xg, key_value_weight[0], preferred_element_type=f32)
        rest = jnp.concatenate([rest.astype(bf16), second.astype(bf16), sq_hi, sq_lo], axis=1)
        first_y = first_half.reshape(n_z, n_y, own_rows, cut).transpose(1, 0, 2, 3)
        first_z = rest.reshape(n_z, n_y, own_rows, rest.shape[1])
        part_a = sum(r.astype(f32) for r in spread(first_y, y_pos, along_y)).astype(bf16)
        part_b = sum(r.astype(f32) for r in spread(first_z, z_pos, along_z))
        total_a = sum(r.astype(f32) for r in spread(part_a, z_pos, along_z))
        total_b = sum(spread(part_b, y_pos, along_y))
        total = jnp.concatenate([total_a, total_b], axis=1)
        total_sq = total[:, query_cols + kv_cols] + total[:, query_cols + kv_cols + 1]
        inv = lax.rsqrt(total_sq / MODEL_WIDTH + 1e-05)[:, None]
        query = (total[:, :query_cols] * inv).astype(bf16)
        keyval = (total[:, query_cols : query_cols + kv_cols] * inv).astype(bf16)
        query_heads = query.reshape(
            slots_local, rounds, DRAFT_BLOCK, kv_local, GROUP_HEADS, HEAD_SIZE
        )
        fresh = keyval.reshape(slots_local, block, kv_local, 2 * HEAD_SIZE).transpose(0, 2, 1, 3)
        s_cache = jnp.einsum(
            "srjhgd,shld->shgrjl", query_heads, cache_local[..., :HEAD_SIZE],
            preferred_element_type=f32,
        ) * scale
        s_fresh = jnp.einsum(
            "srjhgd,shld->shgrjl", query_heads, fresh[..., :HEAD_SIZE],
            preferred_element_type=f32,
        ) * scale
        s_fresh = jnp.where(valid[:, None, None], s_fresh, -1e30)
        scores = jnp.concatenate([s_cache, s_fresh], axis=-1)
        weights = jax.nn.softmax(scores, axis=-1).astype(bf16)
        values = jnp.concatenate([cache_local[..., HEAD_SIZE:], fresh[..., HEAD_SIZE:]], axis=2)
        attended = jnp.einsum(
            "shgrjl,shld->srjhgd", weights, values, preferred_element_type=f32
        )
        attended = attended.astype(bf16).reshape(own_rows, query_cols)
        by_z = jnp.stack([attended] + [along_z(attended, k) for k in range(1, n_z)])
        by_zy = jnp.stack([by_z] + [along_y(by_z, k) for k in range(1, n_y)])
        gathered = by_zy.reshape(-1, query_cols)
        partial = jnp.dot(gathered, w_out[0], preferred_element_type=f32).astype(bf16)
        ext_new = jnp.where(keep[:, None, :, None], fresh, jnp.zeros_like(fresh))
        natural = jnp.take(partial, arrived_at(back_index), axis=0)
        pieces = natural.reshape(rounds, n_tensor, rows_local, width_local).transpose(1, 0, 2, 3)
        mine = sum(r.astype(f32) for r in spread(pieces, tensor, along_tensor))
        x_own = jnp.take(xf, own_index, axis=0).reshape(rounds, rows_local, width_local)
        return (x_own + mine).astype(bf16), ext_new

    arrived = jnp.stack([hidden] + [along_tensor(hidden, k) for k in range(1, n_tensor)])
    src_t = inverse // req_local
    shift_t = (tensor - src_t) % n_tensor
    within = (inverse % req_local) * DRAFT_BLOCK
    arrival_index = (
        ((shift_t[:, None, None] * rounds + rr[None, :, None]) * rows_local)
        + within[:, None, None]
        + jj[None, None, :]
    ).reshape(-1)
    record = None
    ext = None
    for step in range(n_segment):
        x = jnp.take(arrived.reshape(-1, width_local), arrival_index, axis=0)
        rec_new, ext_new = layer(x)
        if step == 0:
            record, ext = rec_new, ext_new
        else:
            active = segment == step
            record = jnp.where(active, rec_new, record)
            ext = jnp.where(active, ext_new, ext)
        if step + 1 < n_segment:
            arrived = handed_on(rec_new, step)
    return (record[None], ext[None])


def solution(mesh):
    in_specs = (
        P(None, "tensor", "batch"),
        P("segment", "batch"),
        P("segment", "batch", "tensor"),
        P("segment", "batch", "tensor"),
        P("segment", "tensor", "batch"),
        P("segment", "batch", "tensor", None, None),
        P(),
        P(),
    )
    out_specs = (P("segment", None, "tensor", "batch"), P("segment", "batch", "tensor", None, None))
    return jax.shard_map(shards, mesh=mesh, in_specs=in_specs, out_specs=out_specs, check_vma=False)
```

```python
import jax
import jax.numpy as jnp
from jax import lax
from jax.sharding import PartitionSpec as P

MODEL_WIDTH = 16384
HEAD_SIZE = 128
DRAFT_BLOCK = 4
DECODE_ROUNDS = 3
GROUP_HEADS = 8


BATCH_INNER = 4


def shifted(x, axis, fn):
    n = lax.axis_size(axis)
    return lax.ppermute(x, axis, [(i, fn(i, n)) for i in range(n)])


def along_tensor(x, k):
    return shifted(x, "tensor", lambda i, n: (i + k) % n)


def along_y(x, k):
    m = BATCH_INNER
    return shifted(x, "batch", lambda i, n: (i // m) * m + (i % m + k) % m)


def along_z(x, k):
    m = BATCH_INNER
    return shifted(x, "batch", lambda i, n: ((i // m + k) % (n // m)) * m + i % m)


def spread(blocks, pos, send):
    m = blocks.shape[0]
    out = [lax.dynamic_index_in_dim(blocks, pos, 0, keepdims=False)]
    for k in range(1, m):
        piece = lax.dynamic_index_in_dim(blocks, (pos + k) % m, 0, keepdims=False)
        out.append(send(piece, k))
    return out


def gather_from(x, pos, m, send):
    out = [x] + [send(x, k) for k in range(1, m)]
    order = (pos - jnp.arange(m)) % m
    return jnp.take(jnp.stack(out), order, axis=0)


def passed_along(block, axis, distance):
    devices = range(lax.axis_size(axis))
    route = [(i - distance, i) for i in devices if i - distance in devices]
    return lax.ppermute(block, axis, route)


def shards(
    hidden, norm_gain, w_query, key_value_weight, w_out, key_value_cache, owner_slot, accepted
):
    f32, bf16 = jnp.float32, jnp.bfloat16
    rounds, rows_local, width_local = hidden.shape
    n_segment = lax.axis_size("segment")
    segment = lax.axis_index("segment")
    tensor = lax.axis_index("tensor")
    group = lax.axis_index("batch")
    requests = owner_slot.shape[0]
    rows_total = requests * DRAFT_BLOCK
    slots_local = key_value_cache.shape[1]
    kv_local = key_value_cache.shape[2]
    query_cols = w_query.shape[2]
    kv_cols = key_value_weight.shape[2]
    block = rounds * DRAFT_BLOCK
    own_rows = slots_local * block
    req_local = rows_local // DRAFT_BLOCK
    scale = HEAD_SIZE ** (-0.5)
    gain = norm_gain[0].astype(f32)
    cache_local = key_value_cache[0]

    onehot = (owner_slot[None, :] == jnp.arange(requests)[:, None]).astype(jnp.int32)
    inverse = jnp.sum(onehot * jnp.arange(requests)[None, :], axis=1)
    acc_slot = jnp.sum(onehot[None] * accepted[:, None, :], axis=2)
    acc_own = lax.dynamic_slice_in_dim(acc_slot, group * slots_local, slots_local, 1)

    rr = jnp.arange(rounds)
    jj = jnp.arange(DRAFT_BLOCK)
    sort_index = (
        rr[None, :, None] * rows_total + inverse[:, None, None] * DRAFT_BLOCK + jj[None, None, :]
    ).reshape(-1)
    own_req = tensor * req_local + jnp.arange(req_local)
    own_index = (
        owner_slot[own_req][None, :, None] * block + rr[:, None, None] * DRAFT_BLOCK + jj[None, None, :]
    ).reshape(-1)

    pos = jnp.arange(block)
    r2 = pos // DRAFT_BLOCK
    place = pos % DRAFT_BLOCK
    acc_pos = acc_own[r2, :].T
    earlier = (r2[None, None, None, :] < rr[None, :, None, None]) & (
        place[None, None, None, :] < acc_pos[:, None, None, :]
    )
    same = (r2[None, :] == rr[:, None])[:, None, :] & (place[None, None, :] <= jj[None, :, None])
    valid = earlier | same[None]
    keep = place[None, :] < acc_pos

    n_tensor = lax.axis_size("tensor")
    n_y = BATCH_INNER
    n_z = lax.axis_size("batch") // n_y
    z_pos = group // n_y
    y_pos = group % n_y

    back_index = (
        owner_slot[None, :, None] * block + rr[:, None, None] * DRAFT_BLOCK + jj[None, None, :]
    ).reshape(-1)

    def arrived_at(s):
        b = s // own_rows
        shift_y = (y_pos - b % n_y) % n_y
        shift_z = (z_pos - b // n_y) % n_z
        return (shift_y * n_z + shift_z) * own_rows + s % own_rows

    def layer(x_sorted, last):
        xf = x_sorted.astype(f32)
        sq = jnp.sum(xf * xf, axis=1, keepdims=True)
        sq_hi = sq.astype(bf16)
        sq_lo = (sq - sq_hi.astype(f32)).astype(bf16)
        xg = (xf * gain[None, :]).astype(bf16)
        cut = (query_cols // 2 + kv_cols // 2) // 128 * 128
        first_half = jnp.dot(xg, w_query[0, :, :cut], preferred_element_type=f32).astype(bf16)
        rest = jnp.dot(xg, w_query[0, :, cut:], preferred_element_type=f32)
        second = jnp.dot(xg, key_value_weight[0], preferred_element_type=f32)
        rest = jnp.concatenate([rest.astype(bf16), second.astype(bf16), sq_hi, sq_lo], axis=1)
        first_y = first_half.reshape(n_z, n_y, own_rows, cut).transpose(1, 0, 2, 3)
        first_z = rest.reshape(n_z, n_y, own_rows, rest.shape[1])
        part_a = sum(r.astype(f32) for r in spread(first_y, y_pos, along_y)).astype(bf16)
        part_b = sum(r.astype(f32) for r in spread(first_z, z_pos, along_z)).astype(bf16)
        total_a = sum(r.astype(f32) for r in spread(part_a, z_pos, along_z))
        total_b = sum(r.astype(f32) for r in spread(part_b, y_pos, along_y))
        total = jnp.concatenate([total_a, total_b], axis=1)
        total_sq = total[:, query_cols + kv_cols] + total[:, query_cols + kv_cols + 1]
        inv = lax.rsqrt(total_sq / MODEL_WIDTH + 1e-05)[:, None]
        query = (total[:, :query_cols] * inv).astype(bf16)
        keyval = (total[:, query_cols : query_cols + kv_cols] * inv).astype(bf16)
        query_heads = query.reshape(
            slots_local, rounds, DRAFT_BLOCK, kv_local, GROUP_HEADS, HEAD_SIZE
        )
        fresh = keyval.reshape(slots_local, block, kv_local, 2 * HEAD_SIZE).transpose(0, 2, 1, 3)
        s_cache = jnp.einsum(
            "srjhgd,shld->shgrjl", query_heads, cache_local[..., :HEAD_SIZE],
            preferred_element_type=f32,
        ) * scale
        s_fresh = jnp.einsum(
            "srjhgd,shld->shgrjl", query_heads, fresh[..., :HEAD_SIZE],
            preferred_element_type=f32,
        ) * scale
        s_fresh = jnp.where(valid[:, None, None], s_fresh, -1e30)
        scores = jnp.concatenate([s_cache, s_fresh], axis=-1)
        weights = jax.nn.softmax(scores, axis=-1).astype(bf16)
        values = jnp.concatenate([cache_local[..., HEAD_SIZE:], fresh[..., HEAD_SIZE:]], axis=2)
        attended = jnp.einsum(
            "shgrjl,shld->srjhgd", weights, values, preferred_element_type=f32
        )
        attended = attended.astype(bf16).reshape(own_rows, query_cols)
        by_z = jnp.stack([attended] + [along_z(attended, k) for k in range(1, n_z)])
        by_zy = jnp.stack([by_z] + [along_y(by_z, k) for k in range(1, n_y)])
        gathered = by_zy.reshape(-1, query_cols)
        partial = jnp.dot(gathered, w_out[0], preferred_element_type=f32).astype(bf16)
        ext_new = jnp.where(keep[:, None, :, None], fresh, jnp.zeros_like(fresh))
        if last:
            natural = jnp.take(partial, arrived_at(back_index), axis=0)
            pieces = natural.reshape(rounds, n_tensor, rows_local, width_local).transpose(1, 0, 2, 3)
            mine = sum(r.astype(f32) for r in spread(pieces, tensor, along_tensor))
            x_own = jnp.take(xf, own_index, axis=0).reshape(rounds, rows_local, width_local)
            return None, (x_own + mine).astype(bf16), ext_new
        quarter = partial.shape[0] // n_tensor
        in_order = jnp.take(partial, arrived_at(jnp.arange(partial.shape[0])), axis=0)
        pieces = in_order.reshape(n_tensor, quarter, width_local)
        mine = sum(r.astype(f32) for r in spread(pieces, tensor, along_tensor))
        x_mine = lax.dynamic_index_in_dim(
            xf.reshape(n_tensor, quarter, width_local), tensor, 0, keepdims=False
        )
        x_mine = (x_mine + mine).astype(bf16)
        x_new = gather_from(x_mine, tensor, n_tensor, along_tensor).reshape(-1, width_local)
        rec_new = jnp.take(x_new, own_index, axis=0).reshape(rounds, rows_local, width_local)
        return x_new, rec_new, ext_new

    arrived = jnp.stack([hidden] + [along_tensor(hidden, k) for k in range(1, n_tensor)])
    arrived = arrived.reshape(-1, width_local)
    src_t = inverse // req_local
    shift_t = (tensor - src_t) % n_tensor
    within = (inverse % req_local) * DRAFT_BLOCK
    arrival_index = (
        ((shift_t[:, None, None] * rounds + rr[None, :, None]) * rows_local)
        + within[:, None, None]
        + jj[None, None, :]
    ).reshape(-1)
    x = jnp.take(arrived, arrival_index, axis=0)
    record = None
    ext = None
    for step in range(n_segment):
        x_new, rec_new, ext_new = layer(x, step + 1 == n_segment)
        if step == 0:
            record, ext = rec_new, ext_new
        else:
            active = segment == step
            record = jnp.where(active, rec_new, record)
            ext = jnp.where(active, ext_new, ext)
        if step + 1 < n_segment:
            x = passed_along(x_new, "segment", 1)
    return (record[None], ext[None])


def solution(mesh):
    in_specs = (
        P(None, "tensor", "batch"),
        P("segment", "batch"),
        P("segment", "batch", "tensor"),
        P("segment", "batch", "tensor"),
        P("segment", "tensor", "batch"),
        P("segment", "batch", "tensor", None, None),
        P(),
        P(),
    )
    out_specs = (P("segment", None, "tensor", "batch"), P("segment", "batch", "tensor", None, None))
    return jax.shard_map(shards, mesh=mesh, in_specs=in_specs, out_specs=out_specs, check_vma=False)
```

```python
import jax
import jax.numpy as jnp
from jax import lax
from jax.sharding import PartitionSpec as P

MODEL_WIDTH = 16384
HEAD_SIZE = 128
DRAFT_BLOCK = 4
DECODE_ROUNDS = 3
GROUP_HEADS = 8


BATCH_INNER = 4


def shifted(x, axis, fn):
    n = lax.axis_size(axis)
    return lax.ppermute(x, axis, [(i, fn(i, n)) for i in range(n)])


def along_tensor(x, k):
    return shifted(x, "tensor", lambda i, n: (i + k) % n)


def along_y(x, k):
    m = BATCH_INNER
    return shifted(x, "batch", lambda i, n: (i // m) * m + (i % m + k) % m)


def along_z(x, k):
    m = BATCH_INNER
    return shifted(x, "batch", lambda i, n: ((i // m + k) % (n // m)) * m + i % m)


def spread(blocks, pos, send):
    m = blocks.shape[0]
    out = [lax.dynamic_index_in_dim(blocks, pos, 0, keepdims=False)]
    for k in range(1, m):
        piece = lax.dynamic_index_in_dim(blocks, (pos + k) % m, 0, keepdims=False)
        out.append(send(piece, k))
    return out


def gather_from(x, pos, m, send):
    out = [x] + [send(x, k) for k in range(1, m)]
    order = (pos - jnp.arange(m)) % m
    return jnp.take(jnp.stack(out), order, axis=0)


def passed_along(block, axis, distance):
    devices = range(lax.axis_size(axis))
    route = [(i - distance, i) for i in devices if i - distance in devices]
    return lax.ppermute(block, axis, route)


def shards(
    hidden, norm_gain, w_query, key_value_weight, w_out, key_value_cache, owner_slot, accepted
):
    f32, bf16 = jnp.float32, jnp.bfloat16
    rounds, rows_local, width_local = hidden.shape
    n_segment = lax.axis_size("segment")
    segment = lax.axis_index("segment")
    tensor = lax.axis_index("tensor")
    group = lax.axis_index("batch")
    requests = owner_slot.shape[0]
    rows_total = requests * DRAFT_BLOCK
    slots_local = key_value_cache.shape[1]
    kv_local = key_value_cache.shape[2]
    query_cols = w_query.shape[2]
    kv_cols = key_value_weight.shape[2]
    block = rounds * DRAFT_BLOCK
    own_rows = slots_local * block
    req_local = rows_local // DRAFT_BLOCK
    scale = HEAD_SIZE ** (-0.5)
    gain = norm_gain[0].astype(f32)
    cache_local = key_value_cache[0]

    onehot = (owner_slot[None, :] == jnp.arange(requests)[:, None]).astype(jnp.int32)
    inverse = jnp.sum(onehot * jnp.arange(requests)[None, :], axis=1)
    acc_slot = jnp.sum(onehot[None] * accepted[:, None, :], axis=2)
    acc_own = lax.dynamic_slice_in_dim(acc_slot, group * slots_local, slots_local, 1)

    rr = jnp.arange(rounds)
    jj = jnp.arange(DRAFT_BLOCK)
    sort_index = (
        rr[None, :, None] * rows_total + inverse[:, None, None] * DRAFT_BLOCK + jj[None, None, :]
    ).reshape(-1)
    own_req = tensor * req_local + jnp.arange(req_local)
    own_index = (
        owner_slot[own_req][None, :, None] * block + rr[:, None, None] * DRAFT_BLOCK + jj[None, None, :]
    ).reshape(-1)

    pos = jnp.arange(block)
    r2 = pos // DRAFT_BLOCK
    place = pos % DRAFT_BLOCK
    acc_pos = acc_own[r2, :].T
    earlier = (r2[None, None, None, :] < rr[None, :, None, None]) & (
        place[None, None, None, :] < acc_pos[:, None, None, :]
    )
    same = (r2[None, :] == rr[:, None])[:, None, :] & (place[None, None, :] <= jj[None, :, None])
    valid = earlier | same[None]
    keep = place[None, :] < acc_pos

    n_tensor = lax.axis_size("tensor")
    n_y = BATCH_INNER
    n_z = lax.axis_size("batch") // n_y
    z_pos = group // n_y
    y_pos = group % n_y

    back_index = (
        owner_slot[None, :, None] * block + rr[:, None, None] * DRAFT_BLOCK + jj[None, None, :]
    ).reshape(-1)

    def arrived_at(s):
        b = s // own_rows
        shift_y = (y_pos - b % n_y) % n_y
        shift_z = (z_pos - b // n_y) % n_z
        return (shift_y * n_z + shift_z) * own_rows + s % own_rows

    def layer(x_sorted, last):
        xf = x_sorted.astype(f32)
        sq = jnp.sum(xf * xf, axis=1, keepdims=True)
        sq_hi = sq.astype(bf16)
        sq_lo = (sq - sq_hi.astype(f32)).astype(bf16)
        xg = (xf * gain[None, :]).astype(bf16)
        cut = (query_cols // 2 + kv_cols // 2) // 128 * 128
        first_half = jnp.dot(xg, w_query[0, :, :cut], preferred_element_type=f32).astype(bf16)
        rest = jnp.dot(xg, w_query[0, :, cut:], preferred_element_type=f32)
        second = jnp.dot(xg, key_value_weight[0], preferred_element_type=f32)
        rest = jnp.concatenate([rest.astype(bf16), second.astype(bf16), sq_hi, sq_lo], axis=1)
        first_y = first_half.reshape(n_z, n_y, own_rows, cut).transpose(1, 0, 2, 3)
        first_z = rest.reshape(n_z, n_y, own_rows, rest.shape[1])
        part_a = sum(r.astype(f32) for r in spread(first_y, y_pos, along_y)).astype(bf16)
        part_b = sum(r.astype(f32) for r in spread(first_z, z_pos, along_z)).astype(bf16)
        total_a = sum(r.astype(f32) for r in spread(part_a, z_pos, along_z))
        total_b = sum(r.astype(f32) for r in spread(part_b, y_pos, along_y))
        total = jnp.concatenate([total_a, total_b], axis=1)
        total_sq = total[:, query_cols + kv_cols] + total[:, query_cols + kv_cols + 1]
        inv = lax.rsqrt(total_sq / MODEL_WIDTH + 1e-05)[:, None]
        query = (total[:, :query_cols] * inv).astype(bf16)
        keyval = (total[:, query_cols : query_cols + kv_cols] * inv).astype(bf16)
        query_heads = query.reshape(
            slots_local, rounds, DRAFT_BLOCK, kv_local, GROUP_HEADS, HEAD_SIZE
        )
        fresh = keyval.reshape(slots_local, block, kv_local, 2 * HEAD_SIZE).transpose(0, 2, 1, 3)
        s_cache = jnp.einsum(
            "srjhgd,shld->shgrjl", query_heads, cache_local[..., :HEAD_SIZE],
            preferred_element_type=f32,
        ) * scale
        s_fresh = jnp.einsum(
            "srjhgd,shld->shgrjl", query_heads, fresh[..., :HEAD_SIZE],
            preferred_element_type=f32,
        ) * scale
        s_fresh = jnp.where(valid[:, None, None], s_fresh, -1e30)
        scores = jnp.concatenate([s_cache, s_fresh], axis=-1)
        weights = jax.nn.softmax(scores, axis=-1).astype(bf16)
        values = jnp.concatenate([cache_local[..., HEAD_SIZE:], fresh[..., HEAD_SIZE:]], axis=2)
        attended = jnp.einsum(
            "shgrjl,shld->srjhgd", weights, values, preferred_element_type=f32
        )
        attended = attended.astype(bf16).reshape(own_rows, query_cols)
        by_z = jnp.stack([attended] + [along_z(attended, k) for k in range(1, n_z)])
        by_zy = jnp.stack([by_z] + [along_y(by_z, k) for k in range(1, n_y)])
        gathered = by_zy.reshape(-1, query_cols)
        partial = jnp.dot(gathered, w_out[0], preferred_element_type=f32).astype(bf16)
        ext_new = jnp.where(keep[:, None, :, None], fresh, jnp.zeros_like(fresh))
        if last:
            by_group = arrived_at(back_index).reshape(rounds, n_tensor, rows_local)
            by_group = by_group.transpose(1, 0, 2).reshape(-1)
            pieces = jnp.take(partial, by_group, axis=0).reshape(
                n_tensor, rounds, rows_local, width_local
            )
            mine = sum(r.astype(f32) for r in spread(pieces, tensor, along_tensor))
            x_own = jnp.take(xf, own_index, axis=0).reshape(rounds, rows_local, width_local)
            return None, (x_own + mine).astype(bf16), ext_new
        quarter = partial.shape[0] // n_tensor
        in_order = jnp.take(partial, arrived_at(jnp.arange(partial.shape[0])), axis=0)
        pieces = in_order.reshape(n_tensor, quarter, width_local)
        mine = sum(r.astype(f32) for r in spread(pieces, tensor, along_tensor))
        x_mine = lax.dynamic_index_in_dim(
            xf.reshape(n_tensor, quarter, width_local), tensor, 0, keepdims=False
        )
        x_mine = (x_mine + mine).astype(bf16)
        x_new = gather_from(x_mine, tensor, n_tensor, along_tensor).reshape(-1, width_local)
        rec_new = jnp.take(x_new, own_index, axis=0).reshape(rounds, rows_local, width_local)
        return x_new, rec_new, ext_new

    arrived = jnp.stack([hidden] + [along_tensor(hidden, k) for k in range(1, n_tensor)])
    arrived = arrived.reshape(-1, width_local)
    src_t = inverse // req_local
    shift_t = (tensor - src_t) % n_tensor
    within = (inverse % req_local) * DRAFT_BLOCK
    arrival_index = (
        ((shift_t[:, None, None] * rounds + rr[None, :, None]) * rows_local)
        + within[:, None, None]
        + jj[None, None, :]
    ).reshape(-1)
    x = jnp.take(arrived, arrival_index, axis=0)
    record = None
    ext = None
    for step in range(n_segment):
        x_new, rec_new, ext_new = layer(x, step + 1 == n_segment)
        if step == 0:
            record, ext = rec_new, ext_new
        else:
            active = segment == step
            record = jnp.where(active, rec_new, record)
            ext = jnp.where(active, ext_new, ext)
        if step + 1 < n_segment:
            x = passed_along(x_new, "segment", 1)
    return (record[None], ext[None])


def solution(mesh):
    in_specs = (
        P(None, "tensor", "batch"),
        P("segment", "batch"),
        P("segment", "batch", "tensor"),
        P("segment", "batch", "tensor"),
        P("segment", "tensor", "batch"),
        P("segment", "batch", "tensor", None, None),
        P(),
        P(),
    )
    out_specs = (P("segment", None, "tensor", "batch"), P("segment", "batch", "tensor", None, None))
    return jax.shard_map(shards, mesh=mesh, in_specs=in_specs, out_specs=out_specs, check_vma=False)
```

```python
import jax
import jax.numpy as jnp
from jax import lax
from jax.sharding import PartitionSpec as P

MODEL_WIDTH = 16384
HEAD_SIZE = 128
DRAFT_BLOCK = 4
DECODE_ROUNDS = 3
GROUP_HEADS = 8


BATCH_INNER = 4


def shifted(x, axis, fn):
    n = lax.axis_size(axis)
    return lax.ppermute(x, axis, [(i, fn(i, n)) for i in range(n)])


def along_tensor(x, k):
    return shifted(x, "tensor", lambda i, n: (i + k) % n)


def along_y(x, k):
    m = BATCH_INNER
    return shifted(x, "batch", lambda i, n: (i // m) * m + (i % m + k) % m)


def along_z(x, k):
    m = BATCH_INNER
    return shifted(x, "batch", lambda i, n: ((i // m + k) % (n // m)) * m + i % m)


def spread(blocks, pos, send):
    m = blocks.shape[0]
    out = [lax.dynamic_index_in_dim(blocks, pos, 0, keepdims=False)]
    for k in range(1, m):
        piece = lax.dynamic_index_in_dim(blocks, (pos + k) % m, 0, keepdims=False)
        out.append(send(piece, k))
    return out


def gather_from(x, pos, m, send):
    out = [x] + [send(x, k) for k in range(1, m)]
    order = (pos - jnp.arange(m)) % m
    return jnp.take(jnp.stack(out), order, axis=0)


def passed_along(block, axis, distance):
    devices = range(lax.axis_size(axis))
    route = [(i - distance, i) for i in devices if i - distance in devices]
    return lax.ppermute(block, axis, route)


def shards(
    hidden, norm_gain, w_query, key_value_weight, w_out, key_value_cache, owner_slot, accepted
):
    f32, bf16 = jnp.float32, jnp.bfloat16
    rounds, rows_local, width_local = hidden.shape
    n_segment = lax.axis_size("segment")
    segment = lax.axis_index("segment")
    tensor = lax.axis_index("tensor")
    group = lax.axis_index("batch")
    requests = owner_slot.shape[0]
    rows_total = requests * DRAFT_BLOCK
    slots_local = key_value_cache.shape[1]
    kv_local = key_value_cache.shape[2]
    query_cols = w_query.shape[2]
    kv_cols = key_value_weight.shape[2]
    block = rounds * DRAFT_BLOCK
    own_rows = slots_local * block
    req_local = rows_local // DRAFT_BLOCK
    scale = HEAD_SIZE ** (-0.5)
    gain = norm_gain[0].astype(f32)
    cache_local = key_value_cache[0]

    onehot = (owner_slot[None, :] == jnp.arange(requests)[:, None]).astype(jnp.int32)
    inverse = jnp.sum(onehot * jnp.arange(requests)[None, :], axis=1)
    acc_slot = jnp.sum(onehot[None] * accepted[:, None, :], axis=2)
    acc_own = lax.dynamic_slice_in_dim(acc_slot, group * slots_local, slots_local, 1)

    rr = jnp.arange(rounds)
    jj = jnp.arange(DRAFT_BLOCK)
    sort_index = (
        rr[None, :, None] * rows_total + inverse[:, None, None] * DRAFT_BLOCK + jj[None, None, :]
    ).reshape(-1)
    own_req = tensor * req_local + jnp.arange(req_local)
    own_index = (
        owner_slot[own_req][None, :, None] * block + rr[:, None, None] * DRAFT_BLOCK + jj[None, None, :]
    ).reshape(-1)

    pos = jnp.arange(block)
    r2 = pos // DRAFT_BLOCK
    place = pos % DRAFT_BLOCK
    acc_pos = acc_own[r2, :].T
    earlier = (r2[None, None, None, :] < rr[None, :, None, None]) & (
        place[None, None, None, :] < acc_pos[:, None, None, :]
    )
    same = (r2[None, :] == rr[:, None])[:, None, :] & (place[None, None, :] <= jj[None, :, None])
    valid = earlier | same[None]
    keep = place[None, :] < acc_pos

    n_tensor = lax.axis_size("tensor")
    n_y = BATCH_INNER
    n_z = lax.axis_size("batch") // n_y
    z_pos = group // n_y
    y_pos = group % n_y

    back_index = (
        owner_slot[None, :, None] * block + rr[:, None, None] * DRAFT_BLOCK + jj[None, None, :]
    ).reshape(-1)

    def arrived_at(s):
        b = s // own_rows
        shift_y = (y_pos - b % n_y) % n_y
        shift_z = (z_pos - b // n_y) % n_z
        return (shift_z * n_y + shift_y) * own_rows + s % own_rows

    def layer(x_sorted, last):
        xf = x_sorted.astype(f32)
        sq = jnp.sum(xf * xf, axis=1, keepdims=True)
        sq_hi = sq.astype(bf16)
        sq_lo = (sq - sq_hi.astype(f32)).astype(bf16)
        xg = (xf * gain[None, :]).astype(bf16)
        cut = (query_cols // 2 + kv_cols // 2) // 128 * 128
        first_half = jnp.dot(xg, w_query[0, :, :cut], preferred_element_type=f32).astype(bf16)
        rest = jnp.dot(xg, w_query[0, :, cut:], preferred_element_type=f32)
        second = jnp.dot(xg, key_value_weight[0], preferred_element_type=f32)
        rest = jnp.concatenate([rest.astype(bf16), second.astype(bf16), sq_hi, sq_lo], axis=1)
        first_y = first_half.reshape(n_z, n_y, own_rows, cut).transpose(1, 0, 2, 3)
        first_z = rest.reshape(n_z, n_y, own_rows, rest.shape[1])
        part_a = sum(r.astype(f32) for r in spread(first_y, y_pos, along_y)).astype(bf16)
        part_b = sum(r.astype(f32) for r in spread(first_z, z_pos, along_z)).astype(bf16)
        total_a = sum(r.astype(f32) for r in spread(part_a, z_pos, along_z))
        total_b = sum(r.astype(f32) for r in spread(part_b, y_pos, along_y))
        total = jnp.concatenate([total_a, total_b], axis=1)
        total_sq = total[:, query_cols + kv_cols] + total[:, query_cols + kv_cols + 1]
        inv = lax.rsqrt(total_sq / MODEL_WIDTH + 1e-05)[:, None]
        query = (total[:, :query_cols] * inv).astype(bf16)
        keyval = (total[:, query_cols : query_cols + kv_cols] * inv).astype(bf16)
        query_heads = query.reshape(
            slots_local, rounds, DRAFT_BLOCK, kv_local, GROUP_HEADS, HEAD_SIZE
        )
        fresh = keyval.reshape(slots_local, block, kv_local, 2 * HEAD_SIZE).transpose(0, 2, 1, 3)
        s_cache = jnp.einsum(
            "srjhgd,shld->shgrjl", query_heads, cache_local[..., :HEAD_SIZE],
            preferred_element_type=f32,
        ) * scale
        s_fresh = jnp.einsum(
            "srjhgd,shld->shgrjl", query_heads, fresh[..., :HEAD_SIZE],
            preferred_element_type=f32,
        ) * scale
        s_fresh = jnp.where(valid[:, None, None], s_fresh, -1e30)
        scores = jnp.concatenate([s_cache, s_fresh], axis=-1)
        weights = jax.nn.softmax(scores, axis=-1).astype(bf16)
        values = jnp.concatenate([cache_local[..., HEAD_SIZE:], fresh[..., HEAD_SIZE:]], axis=2)
        attended = jnp.einsum(
            "shgrjl,shld->srjhgd", weights, values, preferred_element_type=f32
        )
        attended = attended.astype(bf16).reshape(own_rows, query_cols)
        by_y = jnp.stack([attended] + [along_y(attended, k) for k in range(1, n_y)])
        by_zy = jnp.stack([by_y] + [along_z(by_y, k) for k in range(1, n_z)])
        gathered = by_zy.reshape(-1, query_cols)
        partial = jnp.dot(gathered, w_out[0], preferred_element_type=f32).astype(bf16)
        ext_new = jnp.where(keep[:, None, :, None], fresh, jnp.zeros_like(fresh))
        if last:
            natural = jnp.take(partial, arrived_at(back_index), axis=0)
            pieces = natural.reshape(rounds, n_tensor, rows_local, width_local).transpose(1, 0, 2, 3)
            mine = sum(r.astype(f32) for r in spread(pieces, tensor, along_tensor))
            x_own = jnp.take(xf, own_index, axis=0).reshape(rounds, rows_local, width_local)
            return None, (x_own + mine).astype(bf16), ext_new
        quarter = partial.shape[0] // n_tensor
        in_order = jnp.take(partial, arrived_at(jnp.arange(partial.shape[0])), axis=0)
        pieces = in_order.reshape(n_tensor, quarter, width_local)
        mine = sum(r.astype(f32) for r in spread(pieces, tensor, along_tensor))
        x_mine = lax.dynamic_index_in_dim(
            xf.reshape(n_tensor, quarter, width_local), tensor, 0, keepdims=False
        )
        x_mine = (x_mine + mine).astype(bf16)
        x_new = gather_from(x_mine, tensor, n_tensor, along_tensor).reshape(-1, width_local)
        rec_new = jnp.take(x_new, own_index, axis=0).reshape(rounds, rows_local, width_local)
        return x_new, rec_new, ext_new

    arrived = jnp.stack([hidden] + [along_tensor(hidden, k) for k in range(1, n_tensor)])
    arrived = arrived.reshape(-1, width_local)
    src_t = inverse // req_local
    shift_t = (tensor - src_t) % n_tensor
    within = (inverse % req_local) * DRAFT_BLOCK
    arrival_index = (
        ((shift_t[:, None, None] * rounds + rr[None, :, None]) * rows_local)
        + within[:, None, None]
        + jj[None, None, :]
    ).reshape(-1)
    x = jnp.take(arrived, arrival_index, axis=0)
    record = None
    ext = None
    for step in range(n_segment):
        x_new, rec_new, ext_new = layer(x, step + 1 == n_segment)
        if step == 0:
            record, ext = rec_new, ext_new
        else:
            active = segment == step
            record = jnp.where(active, rec_new, record)
            ext = jnp.where(active, ext_new, ext)
        if step + 1 < n_segment:
            x = passed_along(x_new, "segment", 1)
    return (record[None], ext[None])


def solution(mesh):
    in_specs = (
        P(None, "tensor", "batch"),
        P("segment", "batch"),
        P("segment", "batch", "tensor"),
        P("segment", "batch", "tensor"),
        P("segment", "tensor", "batch"),
        P("segment", "batch", "tensor", None, None),
        P(),
        P(),
    )
    out_specs = (P("segment", None, "tensor", "batch"), P("segment", "batch", "tensor", None, None))
    return jax.shard_map(shards, mesh=mesh, in_specs=in_specs, out_specs=out_specs, check_vma=False)
```

```python
import jax
import jax.numpy as jnp
from jax import lax
from jax.sharding import PartitionSpec as P

MODEL_WIDTH = 16384
HEAD_SIZE = 128
DRAFT_BLOCK = 4
DECODE_ROUNDS = 3
GROUP_HEADS = 8


BATCH_INNER = 4


def shifted(x, axis, fn):
    n = lax.axis_size(axis)
    return lax.ppermute(x, axis, [(i, fn(i, n)) for i in range(n)])


def along_tensor(x, k):
    return shifted(x, "tensor", lambda i, n: (i + k) % n)


def along_y(x, k):
    m = BATCH_INNER
    return shifted(x, "batch", lambda i, n: (i // m) * m + (i % m + k) % m)


def along_z(x, k):
    m = BATCH_INNER
    return shifted(x, "batch", lambda i, n: ((i // m + k) % (n // m)) * m + i % m)


def spread(blocks, pos, send):
    m = blocks.shape[0]
    out = [lax.dynamic_index_in_dim(blocks, pos, 0, keepdims=False)]
    for k in range(1, m):
        piece = lax.dynamic_index_in_dim(blocks, (pos + k) % m, 0, keepdims=False)
        out.append(send(piece, k))
    return out


def gather_from(x, pos, m, send):
    out = [x] + [send(x, k) for k in range(1, m)]
    order = (pos - jnp.arange(m)) % m
    return jnp.take(jnp.stack(out), order, axis=0)


def passed_along(block, axis, distance):
    devices = range(lax.axis_size(axis))
    route = [(i - distance, i) for i in devices if i - distance in devices]
    return lax.ppermute(block, axis, route)


def shards(
    hidden, norm_gain, w_query, key_value_weight, w_out, key_value_cache, owner_slot, accepted
):
    f32, bf16 = jnp.float32, jnp.bfloat16
    rounds, rows_local, width_local = hidden.shape
    n_segment = lax.axis_size("segment")
    segment = lax.axis_index("segment")
    tensor = lax.axis_index("tensor")
    group = lax.axis_index("batch")
    requests = owner_slot.shape[0]
    rows_total = requests * DRAFT_BLOCK
    slots_local = key_value_cache.shape[1]
    kv_local = key_value_cache.shape[2]
    query_cols = w_query.shape[2]
    kv_cols = key_value_weight.shape[2]
    block = rounds * DRAFT_BLOCK
    own_rows = slots_local * block
    req_local = rows_local // DRAFT_BLOCK
    scale = HEAD_SIZE ** (-0.5)
    gain = norm_gain[0].astype(f32)
    cache_local = key_value_cache[0]

    onehot = (owner_slot[None, :] == jnp.arange(requests)[:, None]).astype(jnp.int32)
    inverse = jnp.sum(onehot * jnp.arange(requests)[None, :], axis=1)
    acc_slot = jnp.sum(onehot[None] * accepted[:, None, :], axis=2)
    acc_own = lax.dynamic_slice_in_dim(acc_slot, group * slots_local, slots_local, 1)

    rr = jnp.arange(rounds)
    jj = jnp.arange(DRAFT_BLOCK)
    sort_index = (
        rr[None, :, None] * rows_total + inverse[:, None, None] * DRAFT_BLOCK + jj[None, None, :]
    ).reshape(-1)
    own_req = tensor * req_local + jnp.arange(req_local)
    own_index = (
        owner_slot[own_req][None, :, None] * block + rr[:, None, None] * DRAFT_BLOCK + jj[None, None, :]
    ).reshape(-1)

    pos = jnp.arange(block)
    r2 = pos // DRAFT_BLOCK
    place = pos % DRAFT_BLOCK
    acc_pos = acc_own[r2, :].T
    earlier = (r2[None, None, None, :] < rr[None, :, None, None]) & (
        place[None, None, None, :] < acc_pos[:, None, None, :]
    )
    same = (r2[None, :] == rr[:, None])[:, None, :] & (place[None, None, :] <= jj[None, :, None])
    valid = earlier | same[None]
    keep = place[None, :] < acc_pos

    n_tensor = lax.axis_size("tensor")
    n_y = BATCH_INNER
    n_z = lax.axis_size("batch") // n_y
    z_pos = group // n_y
    y_pos = group % n_y

    back_index = (
        owner_slot[None, :, None] * block + rr[:, None, None] * DRAFT_BLOCK + jj[None, None, :]
    ).reshape(-1)

    def arrived_at(s):
        b = s // own_rows
        shift_y = (y_pos - b % n_y) % n_y
        shift_z = (z_pos - b // n_y) % n_z
        return (shift_y * n_z + shift_z) * own_rows + s % own_rows

    def layer(x_sorted, last):
        xf = x_sorted.astype(f32)
        sq = jnp.sum(xf * xf, axis=1, keepdims=True)
        sq_hi = sq.astype(bf16)
        sq_lo = (sq - sq_hi.astype(f32)).astype(bf16)
        xg = (xf * gain[None, :]).astype(bf16)
        cut = (query_cols // 2 + kv_cols // 2) // 128 * 128
        first_half = jnp.dot(xg, w_query[0, :, :cut], preferred_element_type=f32).astype(bf16)
        rest = jnp.dot(xg, w_query[0, :, cut:], preferred_element_type=f32)
        second = jnp.dot(xg, key_value_weight[0], preferred_element_type=f32)
        rest = jnp.concatenate([rest.astype(bf16), second.astype(bf16), sq_hi, sq_lo], axis=1)
        first_y = first_half.reshape(n_z, n_y, own_rows, cut).transpose(1, 0, 2, 3)
        first_z = rest.reshape(n_z, n_y, own_rows, rest.shape[1])
        part_a = sum(r.astype(f32) for r in spread(first_y, y_pos, along_y)).astype(bf16)
        part_b = sum(r.astype(f32) for r in spread(first_z, z_pos, along_z)).astype(bf16)
        total_a = sum(r.astype(f32) for r in spread(part_a, z_pos, along_z))
        total_b = sum(r.astype(f32) for r in spread(part_b, y_pos, along_y))
        total = jnp.concatenate([total_a, total_b], axis=1)
        total_sq = total[:, query_cols + kv_cols] + total[:, query_cols + kv_cols + 1]
        inv = lax.rsqrt(total_sq / MODEL_WIDTH + 1e-05)[:, None]
        query = (total[:, :query_cols] * inv).astype(bf16)
        keyval = (total[:, query_cols : query_cols + kv_cols] * inv).astype(bf16)
        query_heads = query.reshape(
            slots_local, rounds, DRAFT_BLOCK, kv_local, GROUP_HEADS, HEAD_SIZE
        )
        fresh = keyval.reshape(slots_local, block, kv_local, 2 * HEAD_SIZE).transpose(0, 2, 1, 3)
        s_cache = jnp.einsum(
            "srjhgd,shld->shgrjl", query_heads, cache_local[..., :HEAD_SIZE],
            preferred_element_type=f32,
        ) * scale
        s_fresh = jnp.einsum(
            "srjhgd,shld->shgrjl", query_heads, fresh[..., :HEAD_SIZE],
            preferred_element_type=f32,
        ) * scale
        s_fresh = jnp.where(valid[:, None, None], s_fresh, -1e30)
        top = jnp.maximum(
            jnp.max(s_cache, axis=-1, keepdims=True), jnp.max(s_fresh, axis=-1, keepdims=True)
        )
        e_cache = jnp.exp(s_cache - top)
        e_fresh = jnp.exp(s_fresh - top)
        denom = jnp.sum(e_cache, axis=-1, keepdims=True) + jnp.sum(e_fresh, axis=-1, keepdims=True)
        w_cache = (e_cache / denom).astype(bf16)
        w_fresh = (e_fresh / denom).astype(bf16)
        attended = jnp.einsum(
            "shgrjl,shld->srjhgd", w_cache, cache_local[..., HEAD_SIZE:], preferred_element_type=f32
        ) + jnp.einsum(
            "shgrjl,shld->srjhgd", w_fresh, fresh[..., HEAD_SIZE:], preferred_element_type=f32
        )
        attended = attended.astype(bf16).reshape(own_rows, query_cols)
        by_z = jnp.stack([attended] + [along_z(attended, k) for k in range(1, n_z)])
        by_zy = jnp.stack([by_z] + [along_y(by_z, k) for k in range(1, n_y)])
        gathered = by_zy.reshape(-1, query_cols)
        partial = jnp.dot(gathered, w_out[0], preferred_element_type=f32).astype(bf16)
        ext_new = jnp.where(keep[:, None, :, None], fresh, jnp.zeros_like(fresh))
        if last:
            natural = jnp.take(partial, arrived_at(back_index), axis=0)
            pieces = natural.reshape(rounds, n_tensor, rows_local, width_local).transpose(1, 0, 2, 3)
            mine = sum(r.astype(f32) for r in spread(pieces, tensor, along_tensor))
            x_own = jnp.take(xf, own_index, axis=0).reshape(rounds, rows_local, width_local)
            return None, (x_own + mine).astype(bf16), ext_new
        quarter = partial.shape[0] // n_tensor
        in_order = jnp.take(partial, arrived_at(jnp.arange(partial.shape[0])), axis=0)
        pieces = in_order.reshape(n_tensor, quarter, width_local)
        mine = sum(r.astype(f32) for r in spread(pieces, tensor, along_tensor))
        x_mine = lax.dynamic_index_in_dim(
            xf.reshape(n_tensor, quarter, width_local), tensor, 0, keepdims=False
        )
        x_mine = (x_mine + mine).astype(bf16)
        x_new = gather_from(x_mine, tensor, n_tensor, along_tensor).reshape(-1, width_local)
        rec_new = jnp.take(x_new, own_index, axis=0).reshape(rounds, rows_local, width_local)
        return x_new, rec_new, ext_new

    arrived = jnp.stack([hidden] + [along_tensor(hidden, k) for k in range(1, n_tensor)])
    arrived = arrived.reshape(-1, width_local)
    src_t = inverse // req_local
    shift_t = (tensor - src_t) % n_tensor
    within = (inverse % req_local) * DRAFT_BLOCK
    arrival_index = (
        ((shift_t[:, None, None] * rounds + rr[None, :, None]) * rows_local)
        + within[:, None, None]
        + jj[None, None, :]
    ).reshape(-1)
    x = jnp.take(arrived, arrival_index, axis=0)
    record = None
    ext = None
    for step in range(n_segment):
        x_new, rec_new, ext_new = layer(x, step + 1 == n_segment)
        if step == 0:
            record, ext = rec_new, ext_new
        else:
            active = segment == step
            record = jnp.where(active, rec_new, record)
            ext = jnp.where(active, ext_new, ext)
        if step + 1 < n_segment:
            x = passed_along(x_new, "segment", 1)
    return (record[None], ext[None])


def solution(mesh):
    in_specs = (
        P(None, "tensor", "batch"),
        P("segment", "batch"),
        P("segment", "batch", "tensor"),
        P("segment", "batch", "tensor"),
        P("segment", "tensor", "batch"),
        P("segment", "batch", "tensor", None, None),
        P(),
        P(),
    )
    out_specs = (P("segment", None, "tensor", "batch"), P("segment", "batch", "tensor", None, None))
    return jax.shard_map(shards, mesh=mesh, in_specs=in_specs, out_specs=out_specs, check_vma=False)
```
